32 devices in a mesh: grp: 1, tok: 32 (over z, y, x, core).
Axes of the slice: x: 2, y: 2, z: 4, core: 2. Of those that a mesh axis runs over, the one named last changes fastest.
Arguments:
- activations: bfloat16 [65536, 2048], P('tok')
- out_grads: bfloat16 [65536, 512], P('tok')
- v_bank: bfloat16 [2048, 65536], P('tok'), may hold values from -0.125 to 0.125
- u_bank: bfloat16 [512, 65536], P('tok'), may hold values from -0.25 to 0.25
- query_ids: int32 [16], P('grp'), may hold values from 0 to 2047, as said below
Outputs:
- influence: float32 [65536, 16], P('tok', 'grp')
The draws below stay inside these ranges and needn't reach their ends.
Inputs may be any that keep to these rules, and one draw needn't show every extreme that they name: `query_ids`: the ids are distinct; both 0 and 2047 are among them.
All inputs are finite; a program needn't handle non-finite values.
Results may differ from the reference program's by a relative error of at most 0.0003.
Values may be sent and summed in bfloat16 or wider, within the bound.
No kernel may reach another device: no remote copies, remote signals or barrier semaphores. Data moves between devices by JAX's collectives and lax.ppermute only.
A program may use at most 128 MiB of HBM per device.

```python
import jax
import jax.numpy as jnp
from jax import lax

D_IN = 2048
D_OUT = 512
RANK = 32
QUERIES = 16
BANK = 2048
TOK_DEV = 2048
TOKENS = 65536
N_TOK = 32


def rough_rows(key, count, width):
    k_rows, k_cols, k_base = jax.random.split(key, 3)
    rows = jnp.arange(count, dtype=jnp.float32)[:, None]
    row_scale = 10.0 ** (jax.random.uniform(k_rows, (count, 1), jnp.float32) - 0.5)
    col_scale = 10.0 ** (jax.random.uniform(k_cols, (1, width), jnp.float32) - 0.5)
    base = jax.random.normal(k_base, (count, width), jnp.float32)
    trend = jnp.sqrt(1.0 + 2.0 * rows / count)
    return (base * row_scale * col_scale * trend).astype(jnp.bfloat16)


def draw_activations(key, part):
    return rough_rows(jax.random.fold_in(key, 11), TOKENS, D_IN)


def draw_out_grads(key, part):
    return rough_rows(jax.random.fold_in(key, 23), TOKENS, D_OUT)


def draw_query_ids(key, part):
    k_inner, k_order = jax.random.split(jax.random.fold_in(key, 37))
    inner = jax.random.permutation(k_inner, BANK - 2)[:QUERIES - 2] + 1
    ends = jnp.array([0, BANK - 1], dtype=jnp.int32)
    chosen = jnp.concatenate([ends, inner.astype(jnp.int32)])
    order = jax.random.permutation(k_order, QUERIES)
    return chosen[order].astype(jnp.int32)


def block_levels(rng, dims, cuts, low, high):
    def one(axis_at, parts):
        heights = jax.random.uniform(jax.random.fold_in(jax.random.fold_in(rng, 6), axis_at), (parts,), jnp.float32, low / len(cuts), high / len(cuts))
        return jnp.repeat(jnp.exp(heights), dims[axis_at] // parts).reshape((-1,) + (1,) * (len(dims) - axis_at - 1))

    level = one(*cuts[0])
    for cut in cuts[1:]:
        level = level * one(*cut)
    return level


def noise(own_key, shape, deviation, reach, pieces=(), held_as=jnp.bfloat16):
    result = deviation * jax.random.normal(own_key, shape, jnp.float32)
    if pieces:
        result = result * block_levels(own_key, shape, pieces, -0.22, 0.18)
    return jnp.clip(result, -reach, reach).astype(held_as)


def setup_inputs(seed: int = 0, part: int = 0) -> dict:
    streams_of = jax.random.split(jax.random.key(seed), 6)
    part_splits = jax.random.split(jax.random.fold_in(streams_of[5], part), 6)
    activations = draw_activations(jax.random.fold_in(streams_of[5], 71), part)
    out_grads = draw_out_grads(jax.random.fold_in(streams_of[5], 71), part)
    v_bank = noise(streams_of[2], (D_IN, BANK * RANK), D_IN ** -0.5, 0.125, ((0, 32),))
    u_bank = noise(streams_of[3], (D_OUT, BANK * RANK), D_OUT ** -0.5, 0.25, ((0, 32),))
    query_ids = draw_query_ids(jax.random.fold_in(jax.random.fold_in(streams_of[5], part), 71), part)
    return dict(activations=activations, out_grads=out_grads, v_bank=v_bank, u_bank=u_bank, query_ids=query_ids)


def select_columns(bank, query_ids):
    rows = bank.shape[0]
    shaped = bank.reshape(rows, BANK, RANK)
    picked = jnp.take(shaped, query_ids.astype(jnp.int32), axis=1)
    return picked.reshape(rows, QUERIES * RANK)

def reference(activations, out_grads, v_bank, u_bank, query_ids):
    v_sel = select_columns(v_bank, query_ids)
    u_sel = select_columns(u_bank, query_ids)
    act_blocks = activations.reshape(N_TOK, TOK_DEV, D_IN)
    grad_blocks = out_grads.reshape(N_TOK, TOK_DEV, D_OUT)

    def score_block(pair):
        left, right = pair
        proj_in = jnp.dot(left, v_sel, preferred_element_type=jnp.float32)
        proj_out = jnp.dot(right, u_sel, preferred_element_type=jnp.float32)
        return (proj_in * proj_out).reshape(TOK_DEV, QUERIES, RANK).sum(axis=2)
    scores = lax.map(score_block, (act_blocks, grad_blocks)).reshape(TOKENS, QUERIES)
    scale = jnp.sqrt(lax.optimization_barrier(jnp.sum(scores * scores, axis=0)) / TOKENS + 1e-06)
    return scores / scale[None, :]
```

```python
import jax
import jax.numpy as jnp
from jax import lax
from jax.sharding import PartitionSpec as P

RANK = 32


def select_columns(bank, query_ids):
    pieces = [
        lax.dynamic_slice_in_dim(bank, query_ids[q] * RANK, RANK, axis=1)
        for q in range(query_ids.shape[0])
    ]
    return jnp.concatenate(pieces, axis=1)


def folder(left, piece):
    return jnp.dot(left, piece, preferred_element_type=jnp.float32)


def total_over(x, axis):
    n = lax.axis_size(axis)
    copies = jnp.broadcast_to(x[None], (n,) + x.shape)
    return lax.all_to_all(copies, axis, 0, 0, tiled=False).sum(axis=0)


def on_device(activations, out_grads, v_bank, u_bank, query_ids):
    tok_rows = activations.shape[0]
    queries = query_ids.shape[0]
    v_sel = select_columns(v_bank, query_ids)
    u_sel = select_columns(u_bank, query_ids)
    proj_in = folder(activations, lax.all_gather(v_sel, "tok", axis=0, tiled=True))
    proj_out = folder(out_grads, lax.all_gather(u_sel, "tok", axis=0, tiled=True))
    scores = (proj_in * proj_out).reshape(tok_rows, queries, RANK).sum(axis=2)
    total = total_over(jnp.sum(scores * scores, axis=0), "tok")
    count = tok_rows * lax.axis_size("tok")
    scale = jnp.sqrt(total / count + 1e-06)
    return scores / scale[None, :]


def solution(mesh):
    return jax.shard_map(
        on_device,
        mesh=mesh,
        in_specs=(P("tok", None), P("tok", None), P("tok", None), P("tok", None), P("grp")),
        out_specs=P("tok", "grp"),
        check_vma=False,
    )
```

```python
import jax
import jax.numpy as jnp
from jax import lax
from jax.sharding import PartitionSpec as P
from jax.experimental import pallas as pl
from jax.experimental.pallas import tpu as pltpu

RANK = 32
LANES = 128
PER_TILE = LANES // RANK


def pick_kernel(ids_ref, bank_ref, out_ref, buf, sems):
    g = pl.program_id(0)
    rows = out_ref.shape[0]
    copies = []
    for j in range(PER_TILE):
        qid = ids_ref[g * PER_TILE + j]
        tile = jnp.minimum(jnp.maximum(qid // PER_TILE, 0), bank_ref.shape[1] // LANES - 1)
        start = pl.multiple_of(tile * LANES, LANES)
        copy = pltpu.make_async_copy(bank_ref.at[:, pl.ds(start, LANES)], buf.at[j], sems.at[j])
        copy.start()
        copies.append(copy)
    lane = lax.broadcasted_iota(jnp.int32, (rows, LANES), 1)
    acc = jnp.zeros((rows, LANES), jnp.float32)
    for j in range(PER_TILE):
        copies[j].wait()
        x = buf[j].astype(jnp.float32)
        off = (ids_ref[g * PER_TILE + j] % PER_TILE) * RANK
        shift = (RANK * j - off + LANES) % LANES
        moved = x
        for s in range(RANK, LANES, RANK):
            moved = jnp.where(shift == s, pltpu.roll(x, s, 1), moved)
        keep = (lane >= RANK * j) & (lane < RANK * (j + 1))
        acc = jnp.where(keep, moved, acc)
    out_ref[...] = acc.astype(out_ref.dtype)


def pick_columns(bank, query_ids):
    rows = bank.shape[0]
    queries = query_ids.shape[0]
    assert queries % PER_TILE == 0
    return pl.pallas_call(
        pick_kernel,
        out_shape=jax.ShapeDtypeStruct((rows, queries * RANK), bank.dtype),
        grid_spec=pltpu.PrefetchScalarGridSpec(
            num_scalar_prefetch=1,
            grid=(queries // PER_TILE,),
            in_specs=[pl.BlockSpec(memory_space=pl.ANY)],
            out_specs=pl.BlockSpec((rows, LANES), lambda g, ids: (0, g)),
            scratch_shapes=[pltpu.VMEM((PER_TILE, rows, LANES), bank.dtype), pltpu.SemaphoreType.DMA((PER_TILE,))],
        ),
    )(query_ids, bank)


def folder(left, piece):
    return jnp.dot(left, piece, preferred_element_type=jnp.float32)


def total_over(x, axis):
    n = lax.axis_size(axis)
    copies = jnp.broadcast_to(x[None], (n,) + x.shape)
    return lax.all_to_all(copies, axis, 0, 0, tiled=False).sum(axis=0)


def on_device(activations, out_grads, v_bank, u_bank, query_ids):
    tok_rows = activations.shape[0]
    queries = query_ids.shape[0]
    v_sel = pick_columns(v_bank, query_ids)
    u_sel = pick_columns(u_bank, query_ids)
    proj_in = folder(activations, lax.all_gather(v_sel, "tok", axis=0, tiled=True))
    proj_out = folder(out_grads, lax.all_gather(u_sel, "tok", axis=0, tiled=True))
    scores = (proj_in * proj_out).reshape(tok_rows, queries, RANK).sum(axis=2)
    total = total_over(jnp.sum(scores * scores, axis=0), "tok")
    count = tok_rows * lax.axis_size("tok")
    scale = jnp.sqrt(total / count + 1e-06)
    return scores / scale[None, :]


def solution(mesh):
    return jax.shard_map(
        on_device,
        mesh=mesh,
        in_specs=(P("tok", None), P("tok", None), P("tok", None), P("tok", None), P("grp")),
        out_specs=P("tok", "grp"),
        check_vma=False,
    )
```

```python
import jax
import jax.numpy as jnp
from jax import lax
from jax.sharding import Mesh, PartitionSpec as P
from jax.experimental import pallas as pl
from jax.experimental.pallas import tpu as pltpu

RANK = 32
LANES = 128
PER_TILE = LANES // RANK


def pick_kernel(ids_ref, v_ref, u_ref, v_out, u_out, v_buf, u_buf, sems):
    queries = ids_ref.shape[0]
    copies = []
    for k, (bank, buf) in enumerate(((v_ref, v_buf), (u_ref, u_buf))):
        last = bank.shape[1] // LANES - 1
        for q in range(queries):
            tile = jnp.minimum(jnp.maximum(ids_ref[q] // PER_TILE, 0), last)
            start = pl.multiple_of(tile * LANES, LANES)
            copy = pltpu.make_async_copy(bank.at[:, pl.ds(start, LANES)], buf.at[q], sems.at[k, q])
            copy.start()
            copies.append(copy)
    for k, (buf, out) in enumerate(((v_buf, v_out), (u_buf, u_out))):
        rows = out.shape[0]
        lane = lax.broadcasted_iota(jnp.int32, (rows, LANES), 1)
        for g in range(queries // PER_TILE):
            acc = jnp.zeros((rows, LANES), jnp.float32)
            for j in range(PER_TILE):
                q = g * PER_TILE + j
                copies[k * queries + q].wait()
                x = buf[q].astype(jnp.float32)
                off = (ids_ref[q] % PER_TILE) * RANK
                shift = (RANK * j - off + LANES) % LANES
                moved = x
                for s in range(RANK, LANES, RANK):
                    moved = jnp.where(shift == s, pltpu.roll(x, s, 1), moved)
                keep = (lane >= RANK * j) & (lane < RANK * (j + 1))
                acc = jnp.where(keep, moved, acc)
            out[:, g * LANES:(g + 1) * LANES] = acc.astype(out.dtype)


def pick_columns(v_bank, u_bank, query_ids):
    queries = query_ids.shape[0]
    assert queries % PER_TILE == 0
    vmem = pl.BlockSpec(memory_space=pltpu.VMEM)
    return pl.pallas_call(
        pick_kernel,
        out_shape=(
            jax.ShapeDtypeStruct((v_bank.shape[0], queries * RANK), v_bank.dtype),
            jax.ShapeDtypeStruct((u_bank.shape[0], queries * RANK), u_bank.dtype),
        ),
        in_specs=[
            pl.BlockSpec(memory_space=pltpu.SMEM),
            pl.BlockSpec(memory_space=pl.ANY),
            pl.BlockSpec(memory_space=pl.ANY),
        ],
        out_specs=(vmem, vmem),
        scratch_shapes=[
            pltpu.VMEM((queries, v_bank.shape[0], LANES), v_bank.dtype),
            pltpu.VMEM((queries, u_bank.shape[0], LANES), u_bank.dtype),
            pltpu.SemaphoreType.DMA((2, queries)),
        ],
    )(query_ids, v_bank, u_bank)


OUTER = "tok_o"
INNER = "tok_i"
TOK = (OUTER, INNER)


def folder(left, piece):
    return jnp.dot(left, piece, preferred_element_type=jnp.float32)


def total_over(x, axis, n):
    copies = jnp.broadcast_to(x[None], (n,) + x.shape)
    return lax.all_to_all(copies, axis, 0, 0, tiled=False).sum(axis=0)


def gather_factors(v_sel, u_sel):
    rows_v = v_sel.shape[0]
    both = jnp.concatenate([v_sel, u_sel], axis=0)
    held = lax.all_gather(both, OUTER, axis=0, tiled=False)
    held = lax.all_gather(held, INNER, axis=0, tiled=False)
    held = jnp.swapaxes(held, 0, 1)
    cols = both.shape[1]
    return held[:, :, :rows_v].reshape(-1, cols), held[:, :, rows_v:].reshape(-1, cols)


def on_device(activations, out_grads, v_bank, u_bank, query_ids):
    tok_rows = activations.shape[0]
    queries = query_ids.shape[0]
    n = lax.axis_size(OUTER) * lax.axis_size(INNER)
    v_sel, u_sel = pick_columns(v_bank, u_bank, query_ids)
    v_full, u_full = gather_factors(v_sel, u_sel)
    proj_in = folder(activations, v_full)
    proj_out = folder(out_grads, u_full)
    scores = (proj_in * proj_out).reshape(tok_rows, queries, RANK).sum(axis=2)
    total = total_over(jnp.sum(scores * scores, axis=0), TOK, n)
    scale = jnp.sqrt(total / (tok_rows * n) + 1e-06)
    return scores / scale[None, :]


def split_mesh(mesh):
    grp, tok = mesh.devices.shape
    inner = 8 if tok % 8 == 0 and tok > 8 else tok
    return Mesh(mesh.devices.reshape(grp, tok // inner, inner), ("grp", OUTER, INNER))


def solution(mesh):
    rows = P(TOK, None)
    return jax.shard_map(
        on_device,
        mesh=split_mesh(mesh),
        in_specs=(rows, rows, rows, rows, P("grp")),
        out_specs=P(TOK, "grp"),
        check_vma=False,
    )
```

```python
import jax
import jax.numpy as jnp
from jax import lax
from jax.sharding import Mesh, PartitionSpec as P
from jax.experimental import pallas as pl
from jax.experimental.pallas import tpu as pltpu

RANK = 32
LANES = 128
PER_TILE = LANES // RANK


def pick_kernel(ids_ref, v_ref, u_ref, v_out, u_out, v_buf, u_buf, sems):
    queries = ids_ref.shape[0]
    copies = []
    for k, (bank, buf) in enumerate(((v_ref, v_buf), (u_ref, u_buf))):
        last = bank.shape[1] // LANES - 1
        for q in range(queries):
            tile = jnp.minimum(jnp.maximum(ids_ref[q] // PER_TILE, 0), last)
            start = pl.multiple_of(tile * LANES, LANES)
            copy = pltpu.make_async_copy(bank.at[:, pl.ds(start, LANES)], buf.at[q], sems.at[k, q])
            copy.start()
            copies.append(copy)
    for k, (buf, out) in enumerate(((v_buf, v_out), (u_buf, u_out))):
        rows = out.shape[0]
        lane = lax.broadcasted_iota(jnp.int32, (rows, LANES), 1)
        for g in range(queries // PER_TILE):
            acc = jnp.zeros((rows, LANES), jnp.float32)
            for j in range(PER_TILE):
                q = g * PER_TILE + j
                copies[k * queries + q].wait()
                x = buf[q].astype(jnp.float32)
                off = (ids_ref[q] % PER_TILE) * RANK
                shift = (RANK * j - off + LANES) % LANES
                moved = x
                for s in range(RANK, LANES, RANK):
                    moved = jnp.where(shift == s, pltpu.roll(x, s, 1), moved)
                keep = (lane >= RANK * j) & (lane < RANK * (j + 1))
                acc = jnp.where(keep, moved, acc)
            out[:, g * LANES:(g + 1) * LANES] = acc.astype(out.dtype)


def pick_columns(v_bank, u_bank, query_ids):
    queries = query_ids.shape[0]
    assert queries % PER_TILE == 0
    vmem = pl.BlockSpec(memory_space=pltpu.VMEM)
    return pl.pallas_call(
        pick_kernel,
        out_shape=(
            jax.ShapeDtypeStruct((v_bank.shape[0], queries * RANK), v_bank.dtype),
            jax.ShapeDtypeStruct((u_bank.shape[0], queries * RANK), u_bank.dtype),
        ),
        in_specs=[
            pl.BlockSpec(memory_space=pltpu.SMEM),
            pl.BlockSpec(memory_space=pl.ANY),
            pl.BlockSpec(memory_space=pl.ANY),
        ],
        out_specs=(vmem, vmem),
        scratch_shapes=[
            pltpu.VMEM((queries, v_bank.shape[0], LANES), v_bank.dtype),
            pltpu.VMEM((queries, u_bank.shape[0], LANES), u_bank.dtype),
            pltpu.SemaphoreType.DMA((2, queries)),
        ],
    )(query_ids, v_bank, u_bank)


OUTER = "tok_o"
MIDDLE = "tok_m"
CORE = "tok_c"
TOK = (OUTER, MIDDLE, CORE)


def folder(left, piece):
    return jnp.dot(left, piece, preferred_element_type=jnp.float32)


def total_over(x, axis, n):
    copies = jnp.broadcast_to(x[None], (n,) + x.shape)
    return lax.all_to_all(copies, axis, 0, 0, tiled=False).sum(axis=0)


def spread(x, axis):
    k = lax.axis_size(axis)
    copies = jnp.broadcast_to(x[None], (k,) + x.shape)
    return lax.all_to_all(copies, axis, 0, 0, tiled=False)


def gather_factors(v_sel, u_sel):
    rows_v = v_sel.shape[0]
    cols = v_sel.shape[1]
    both = jnp.concatenate([v_sel, u_sel], axis=0)
    held = lax.all_gather(both, OUTER, axis=0, tiled=False)
    held = spread(held, MIDDLE)
    held = spread(held, CORE)
    held = jnp.transpose(held, (2, 1, 0, 3, 4))
    return held[:, :, :, :rows_v].reshape(-1, cols), held[:, :, :, rows_v:].reshape(-1, cols)


def on_device(activations, out_grads, v_bank, u_bank, query_ids):
    tok_rows = activations.shape[0]
    queries = query_ids.shape[0]
    n = lax.axis_size(OUTER) * lax.axis_size(MIDDLE) * lax.axis_size(CORE)
    v_sel, u_sel = pick_columns(v_bank, u_bank, query_ids)
    v_full, u_full = gather_factors(v_sel, u_sel)
    proj_in = folder(activations, v_full)
    proj_out = folder(out_grads, u_full)
    scores = (proj_in * proj_out).reshape(tok_rows, queries, RANK).sum(axis=2)
    total = total_over(jnp.sum(scores * scores, axis=0), TOK, n)
    scale = jnp.sqrt(total / (tok_rows * n) + 1e-06)
    return scores / scale[None, :]


def split_mesh(mesh):
    grp, tok = mesh.devices.shape
    assert tok % 8 == 0
    return Mesh(mesh.devices.reshape(grp, tok // 8, 4, 2), ("grp",) + TOK)


def solution(mesh):
    rows = P(TOK, None)
    return jax.shard_map(
        on_device,
        mesh=split_mesh(mesh),
        in_specs=(rows, rows, rows, rows, P("grp")),
        out_specs=P(TOK, "grp"),
        check_vma=False,
    )
```

```python
import jax
import jax.numpy as jnp
from jax import lax
from jax.sharding import Mesh, PartitionSpec as P
from jax.experimental import pallas as pl
from jax.experimental.pallas import tpu as pltpu

RANK = 32
LANES = 128
PER_TILE = LANES // RANK


def pick_kernel(ids_ref, v_ref, u_ref, out, v_buf, u_buf, sems):
    queries = ids_ref.shape[0]
    copies = []
    for k, (bank, buf) in enumerate(((v_ref, v_buf), (u_ref, u_buf))):
        last = bank.shape[1] // LANES - 1
        for q in range(queries):
            tile = jnp.minimum(jnp.maximum(ids_ref[q] // PER_TILE, 0), last)
            start = pl.multiple_of(tile * LANES, LANES)
            copy = pltpu.make_async_copy(bank.at[:, pl.ds(start, LANES)], buf.at[q], sems.at[k, q])
            copy.start()
            copies.append(copy)
    bases = (0, v_buf.shape[1])
    for k, buf in enumerate((v_buf, u_buf)):
        rows = buf.shape[1]
        base = bases[k]
        lane = lax.broadcasted_iota(jnp.int32, (rows, LANES), 1)
        for g in range(queries // PER_TILE):
            acc = jnp.zeros((rows, LANES), jnp.float32)
            for j in range(PER_TILE):
                q = g * PER_TILE + j
                copies[k * queries + q].wait()
                x = buf[q].astype(jnp.float32)
                off = (ids_ref[q] % PER_TILE) * RANK
                shift = (RANK * j - off + LANES) % LANES
                moved = x
                for s in range(RANK, LANES, RANK):
                    moved = jnp.where(shift == s, pltpu.roll(x, s, 1), moved)
                keep = (lane >= RANK * j) & (lane < RANK * (j + 1))
                acc = jnp.where(keep, moved, acc)
            out[base:base + rows, g * LANES:(g + 1) * LANES] = acc.astype(out.dtype)


def pick_columns(v_bank, u_bank, query_ids):
    queries = query_ids.shape[0]
    assert queries % PER_TILE == 0
    vmem = pl.BlockSpec(memory_space=pltpu.VMEM)
    return pl.pallas_call(
        pick_kernel,
        out_shape=jax.ShapeDtypeStruct((v_bank.shape[0] + u_bank.shape[0], queries * RANK), v_bank.dtype),
        in_specs=[
            pl.BlockSpec(memory_space=pltpu.SMEM),
            pl.BlockSpec(memory_space=pl.ANY),
            pl.BlockSpec(memory_space=pl.ANY),
        ],
        out_specs=vmem,
        scratch_shapes=[
            pltpu.VMEM((queries, v_bank.shape[0], LANES), v_bank.dtype),
            pltpu.VMEM((queries, u_bank.shape[0], LANES), u_bank.dtype),
            pltpu.SemaphoreType.DMA((2, queries)),
        ],
    )(query_ids, v_bank, u_bank)


OUTER = "tok_o"
MIDDLE = "tok_m"
CORE = "tok_c"
TOK = (OUTER, MIDDLE, CORE)


def folder(left, piece):
    return jnp.dot(left, piece, preferred_element_type=jnp.float32)


def total_over(x, axis, n):
    copies = jnp.broadcast_to(x[None], (n,) + x.shape)
    return lax.all_to_all(copies, axis, 0, 0, tiled=False).sum(axis=0)


def spread(x, axis, at):
    k = lax.axis_size(axis)
    copies = jnp.broadcast_to(jnp.expand_dims(x, at), x.shape[:at] + (k,) + x.shape[at:])
    return lax.all_to_all(copies, axis, at, at, tiled=True)


def gather_factors(both, rows_v):
    cols = both.shape[1]
    held = lax.all_gather(both, OUTER, axis=0, tiled=False)
    held = spread(held, MIDDLE, 1)
    held = spread(held, CORE, 2)
    return held[:, :, :, :rows_v].reshape(-1, cols), held[:, :, :, rows_v:].reshape(-1, cols)


def on_device(activations, out_grads, v_bank, u_bank, query_ids):
    tok_rows = activations.shape[0]
    queries = query_ids.shape[0]
    n = lax.axis_size(OUTER) * lax.axis_size(MIDDLE) * lax.axis_size(CORE)
    both = pick_columns(v_bank, u_bank, query_ids)
    v_full, u_full = gather_factors(both, v_bank.shape[0])
    proj_in = folder(activations, v_full)
    proj_out = folder(out_grads, u_full)
    scores = (proj_in * proj_out).reshape(tok_rows, queries, RANK).sum(axis=2)
    total = total_over(jnp.sum(scores * scores, axis=0), TOK, n)
    scale = jnp.sqrt(total / (tok_rows * n) + 1e-06)
    return scores / scale[None, :]


def split_mesh(mesh):
    grp, tok = mesh.devices.shape
    assert tok % 8 == 0
    return Mesh(mesh.devices.reshape(grp, tok // 8, 4, 2), ("grp",) + TOK)


def solution(mesh):
    rows = P(TOK, None)
    return jax.shard_map(
        on_device,
        mesh=split_mesh(mesh),
        in_specs=(rows, rows, rows, rows, P("grp")),
        out_specs=P(TOK, "grp"),
        check_vma=False,
    )
```

```python
import jax
import jax.numpy as jnp
from jax import lax
from jax.sharding import Mesh, PartitionSpec as P
from jax.experimental import pallas as pl
from jax.experimental.pallas import tpu as pltpu

RANK = 32
LANES = 128
PER_TILE = LANES // RANK


def pick_kernel(ids_ref, v_ref, u_ref, out, v_buf, u_buf, sems):
    queries = ids_ref.shape[0]
    copies = []
    for k, (bank, buf) in enumerate(((v_ref, v_buf), (u_ref, u_buf))):
        last = bank.shape[1] // LANES - 1
        for q in range(queries):
            tile = jnp.minimum(jnp.maximum(ids_ref[q] // PER_TILE, 0), last)
            start = pl.multiple_of(tile * LANES, LANES)
            copy = pltpu.make_async_copy(bank.at[:, pl.ds(start, LANES)], buf.at[q], sems.at[k, q])
            copy.start()
            copies.append(copy)
    bases = (0, v_buf.shape[1])
    for k, buf in enumerate((v_buf, u_buf)):
        rows = buf.shape[1]
        base = bases[k]
        lane = lax.broadcasted_iota(jnp.int32, (rows, LANES), 1)
        for g in range(queries // PER_TILE):
            acc = jnp.zeros((rows, LANES), jnp.float32)
            for j in range(PER_TILE):
                q = g * PER_TILE + j
                copies[k * queries + q].wait()
                x = buf[q].astype(jnp.float32)
                off = (ids_ref[q] % PER_TILE) * RANK
                shift = (RANK * j - off + LANES) % LANES
                moved = x
                for s in range(RANK, LANES, RANK):
                    moved = jnp.where(shift == s, pltpu.roll(x, s, 1), moved)
                keep = (lane >= RANK * j) & (lane < RANK * (j + 1))
                acc = jnp.where(keep, moved, acc)
            out[base:base + rows, g * LANES:(g + 1) * LANES] = acc.astype(out.dtype)


def pick_columns(v_bank, u_bank, query_ids):
    queries = query_ids.shape[0]
    assert queries % PER_TILE == 0
    vmem = pl.BlockSpec(memory_space=pltpu.VMEM)
    return pl.pallas_call(
        pick_kernel,
        out_shape=jax.ShapeDtypeStruct((v_bank.shape[0] + u_bank.shape[0], queries * RANK), v_bank.dtype),
        in_specs=[
            pl.BlockSpec(memory_space=pltpu.SMEM),
            pl.BlockSpec(memory_space=pl.ANY),
            pl.BlockSpec(memory_space=pl.ANY),
        ],
        out_specs=vmem,
        scratch_shapes=[
            pltpu.VMEM((queries, v_bank.shape[0], LANES), v_bank.dtype),
            pltpu.VMEM((queries, u_bank.shape[0], LANES), u_bank.dtype),
            pltpu.SemaphoreType.DMA((2, queries)),
        ],
    )(query_ids, v_bank, u_bank)


OUTER = "tok_o"
MIDDLE = "tok_m"
CORE = "tok_c"
TOK = (OUTER, MIDDLE, CORE)


def folder(left, piece):
    return jnp.dot(left, piece, preferred_element_type=jnp.float32)


def total_over(x, axis, n):
    copies = jnp.broadcast_to(x[None], (n,) + x.shape)
    return lax.all_to_all(copies, axis, 0, 0, tiled=False).sum(axis=0)


def spread(x, axis, at):
    k = lax.axis_size(axis)
    copies = jnp.broadcast_to(jnp.expand_dims(x, at), x.shape[:at] + (k,) + x.shape[at:])
    return lax.all_to_all(copies, axis, at, at, tiled=True)


def shifted(x, axis, at):
    k = lax.axis_size(axis)
    if k > 4:
        return spread(x, axis, at)
    me = lax.axis_index(axis)
    got = [x] + [lax.ppermute(x, axis, [(j, (j + s) % k) for j in range(k)]) for s in range(1, k)]
    back = jnp.stack(got[::-1] + got[::-1], axis=at)
    return lax.dynamic_slice_in_dim(back, (k - 1 - me) % k, k, axis=at)


def gather_factors(both, rows_v):
    cols = both.shape[1]
    held = shifted(both, OUTER, 0)
    held = shifted(held, MIDDLE, 1)
    held = spread(held, CORE, 2)
    return held[:, :, :, :rows_v].reshape(-1, cols), held[:, :, :, rows_v:].reshape(-1, cols)


def on_device(activations, out_grads, v_bank, u_bank, query_ids):
    tok_rows = activations.shape[0]
    queries = query_ids.shape[0]
    n = lax.axis_size(OUTER) * lax.axis_size(MIDDLE) * lax.axis_size(CORE)
    both = pick_columns(v_bank, u_bank, query_ids)
    v_full, u_full = gather_factors(both, v_bank.shape[0])
    proj_in = folder(activations, v_full)
    proj_out = folder(out_grads, u_full)
    scores = (proj_in * proj_out).reshape(tok_rows, queries, RANK).sum(axis=2)
    total = total_over(jnp.sum(scores * scores, axis=0), TOK, n)
    scale = jnp.sqrt(total / (tok_rows * n) + 1e-06)
    return scores / scale[None, :]


def split_mesh(mesh):
    grp, tok = mesh.devices.shape
    assert tok % 8 == 0
    return Mesh(mesh.devices.reshape(grp, tok // 8, 4, 2), ("grp",) + TOK)


def solution(mesh):
    rows = P(TOK, None)
    return jax.shard_map(
        on_device,
        mesh=split_mesh(mesh),
        in_specs=(rows, rows, rows, rows, P("grp")),
        out_specs=P(TOK, "grp"),
        check_vma=False,
    )
```

```python
import jax
import jax.numpy as jnp
from jax import lax
from jax.sharding import Mesh, PartitionSpec as P
from jax.experimental import pallas as pl
from jax.experimental.pallas import tpu as pltpu

RANK = 32
LANES = 128
PER_TILE = LANES // RANK


def pick_kernel(ids_ref, v_ref, u_ref, out, v_buf, u_buf, sems):
    queries = ids_ref.shape[0]
    copies = []
    for k, (bank, buf) in enumerate(((v_ref, v_buf), (u_ref, u_buf))):
        last = bank.shape[1] // LANES - 1
        for q in range(queries):
            tile = jnp.minimum(jnp.maximum(ids_ref[q] // PER_TILE, 0), last)
            start = pl.multiple_of(tile * LANES, LANES)
            copy = pltpu.make_async_copy(bank.at[:, pl.ds(start, LANES)], buf.at[q], sems.at[k, q])
            copy.start()
            copies.append(copy)
    bases = (0, v_buf.shape[1])
    for k, buf in enumerate((v_buf, u_buf)):
        rows = buf.shape[1]
        base = bases[k]
        lane = lax.broadcasted_iota(jnp.int32, (rows, LANES), 1)
        for g in range(queries // PER_TILE):
            acc = jnp.zeros((rows, LANES), jnp.float32)
            for j in range(PER_TILE):
                q = g * PER_TILE + j
                copies[k * queries + q].wait()
                x = buf[q].astype(jnp.float32)
                off = (ids_ref[q] % PER_TILE) * RANK
                shift = (RANK * j - off + LANES) % LANES
                moved = pltpu.roll(x, shift, 1)
                keep = (lane >= RANK * j) & (lane < RANK * (j + 1))
                acc = jnp.where(keep, moved, acc)
            out[base:base + rows, g * LANES:(g + 1) * LANES] = acc.astype(out.dtype)


def pick_columns(v_bank, u_bank, query_ids):
    queries = query_ids.shape[0]
    assert queries % PER_TILE == 0
    vmem = pl.BlockSpec(memory_space=pltpu.VMEM)
    return pl.pallas_call(
        pick_kernel,
        out_shape=jax.ShapeDtypeStruct((v_bank.shape[0] + u_bank.shape[0], queries * RANK), v_bank.dtype),
        in_specs=[
            pl.BlockSpec(memory_space=pltpu.SMEM),
            pl.BlockSpec(memory_space=pl.ANY),
            pl.BlockSpec(memory_space=pl.ANY),
        ],
        out_specs=vmem,
        scratch_shapes=[
            pltpu.VMEM((queries, v_bank.shape[0], LANES), v_bank.dtype),
            pltpu.VMEM((queries, u_bank.shape[0], LANES), u_bank.dtype),
            pltpu.SemaphoreType.DMA((2, queries)),
        ],
    )(query_ids, v_bank, u_bank)


OUTER = "tok_o"
MIDDLE = "tok_m"
CORE = "tok_c"
TOK = (OUTER, MIDDLE, CORE)


def folder(left, piece):
    return jnp.dot(left, piece, preferred_element_type=jnp.float32)


def total_over(x, axis, n):
    copies = jnp.broadcast_to(x[None], (n,) + x.shape)
    return lax.all_to_all(copies, axis, 0, 0, tiled=False).sum(axis=0)


def spread(x, axis, at):
    k = lax.axis_size(axis)
    copies = jnp.broadcast_to(jnp.expand_dims(x, at), x.shape[:at] + (k,) + x.shape[at:])
    return lax.all_to_all(copies, axis, at, at, tiled=True)


def shifted(x, axis, at):
    k = lax.axis_size(axis)
    if k > 4:
        return spread(x, axis, at)
    me = lax.axis_index(axis)
    got = [x] + [lax.ppermute(x, axis, [(j, (j + s) % k) for j in range(k)]) for s in range(1, k)]
    back = jnp.stack(got[::-1] + got[::-1], axis=at)
    return lax.dynamic_slice_in_dim(back, (k - 1 - me) % k, k, axis=at)


def gather_factors(both, rows_v):
    cols = both.shape[1]
    held = shifted(both, OUTER, 0)
    held = shifted(held, MIDDLE, 1)
    held = spread(held, CORE, 2)
    return held[:, :, :, :rows_v].reshape(-1, cols), held[:, :, :, rows_v:].reshape(-1, cols)


def on_device(activations, out_grads, v_bank, u_bank, query_ids):
    tok_rows = activations.shape[0]
    queries = query_ids.shape[0]
    n = lax.axis_size(OUTER) * lax.axis_size(MIDDLE) * lax.axis_size(CORE)
    both = pick_columns(v_bank, u_bank, query_ids)
    v_full, u_full = gather_factors(both, v_bank.shape[0])
    proj_in = folder(activations, v_full)
    proj_out = folder(out_grads, u_full)
    scores = (proj_in * proj_out).reshape(tok_rows, queries, RANK).sum(axis=2)
    total = total_over(jnp.sum(scores * scores, axis=0), TOK, n)
    scale = jnp.sqrt(total / (tok_rows * n) + 1e-06)
    return scores / scale[None, :]


def split_mesh(mesh):
    grp, tok = mesh.devices.shape
    assert tok % 8 == 0
    return Mesh(mesh.devices.reshape(grp, tok // 8, 4, 2), ("grp",) + TOK)


def solution(mesh):
    rows = P(TOK, None)
    return jax.shard_map(
        on_device,
        mesh=split_mesh(mesh),
        in_specs=(rows, rows, rows, rows, P("grp")),
        out_specs=P(TOK, "grp"),
        check_vma=False,
    )
```

```python
import jax
import jax.numpy as jnp
from jax import lax
from jax.sharding import Mesh, PartitionSpec as P
from jax.experimental import pallas as pl
from jax.experimental.pallas import tpu as pltpu

RANK = 32
LANES = 128
PER_TILE = LANES // RANK


def pick_kernel(ids_ref, v_ref, u_ref, out, v_buf, u_buf, sems):
    queries = ids_ref.shape[0]
    copies = []
    for k, (bank, buf) in enumerate(((v_ref, v_buf), (u_ref, u_buf))):
        last = bank.shape[1] // LANES - 1
        for q in range(queries):
            tile = jnp.minimum(jnp.maximum(ids_ref[q] // PER_TILE, 0), last)
            start = pl.multiple_of(tile * LANES, LANES)
            copy = pltpu.make_async_copy(bank.at[:, pl.ds(start, LANES)], buf.at[q], sems.at[k, q])
            copy.start()
            copies.append(copy)
    bases = (0, v_buf.shape[1])
    for k, buf in enumerate((v_buf, u_buf)):
        rows = buf.shape[1]
        base = bases[k]
        lane = lax.broadcasted_iota(jnp.int32, (rows, LANES), 1)
        for g in range(queries // PER_TILE):
            acc = jnp.zeros((rows, LANES), jnp.float32)
            for j in range(PER_TILE):
                q = g * PER_TILE + j
                copies[k * queries + q].wait()
                x = buf[q].astype(jnp.float32)
                off = (ids_ref[q] % PER_TILE) * RANK
                shift = (RANK * j - off + LANES) % LANES
                moved = pltpu.roll(x, shift, 1)
                keep = (lane >= RANK * j) & (lane < RANK * (j + 1))
                acc = jnp.where(keep, moved, acc)
            out[base:base + rows, g * LANES:(g + 1) * LANES] = acc.astype(out.dtype)


def pick_columns(v_bank, u_bank, query_ids):
    queries = query_ids.shape[0]
    assert queries % PER_TILE == 0
    vmem = pl.BlockSpec(memory_space=pltpu.VMEM)
    return pl.pallas_call(
        pick_kernel,
        out_shape=jax.ShapeDtypeStruct((v_bank.shape[0] + u_bank.shape[0], queries * RANK), v_bank.dtype),
        in_specs=[
            pl.BlockSpec(memory_space=pltpu.SMEM),
            pl.BlockSpec(memory_space=pl.ANY),
            pl.BlockSpec(memory_space=pl.ANY),
        ],
        out_specs=vmem,
        scratch_shapes=[
            pltpu.VMEM((queries, v_bank.shape[0], LANES), v_bank.dtype),
            pltpu.VMEM((queries, u_bank.shape[0], LANES), u_bank.dtype),
            pltpu.SemaphoreType.DMA((2, queries)),
        ],
    )(query_ids, v_bank, u_bank)


OUTER = "tok_o"
MIDDLE = "tok_m"
CORE = "tok_c"
TOK = (OUTER, MIDDLE, CORE)


def folder(left, piece):
    return jnp.dot(left, piece, preferred_element_type=jnp.float32)


def total_over(x, axis, n):
    copies = jnp.broadcast_to(x[None], (n,) + x.shape)
    return lax.all_to_all(copies, axis, 0, 0, tiled=False).sum(axis=0)


def spread(x, axis, at):
    k = lax.axis_size(axis)
    copies = jnp.broadcast_to(jnp.expand_dims(x, at), x.shape[:at] + (k,) + x.shape[at:])
    return lax.all_to_all(copies, axis, at, at, tiled=True)


def shifted(x, axis, at):
    k = lax.axis_size(axis)
    if k > 4:
        return spread(x, axis, at)
    me = lax.axis_index(axis)
    got = [x] + [lax.ppermute(x, axis, [(j, (j + s) % k) for j in range(k)]) for s in range(1, k)]
    back = jnp.stack(got[::-1] + got[::-1], axis=at)
    return lax.dynamic_slice_in_dim(back, (k - 1 - me) % k, k, axis=at)


def ring_step(x, axis):
    k = lax.axis_size(axis)
    return lax.ppermute(x, axis, [(j, (j + 1) % k) for j in range(k)])


def gather_factors(both, rows_v):
    cols = both.shape[1]
    held = shifted(both, OUTER, 0)
    held = shifted(held, MIDDLE, 1)
    held = spread(held, CORE, 2)
    return held[:, :, :, :rows_v].reshape(-1, cols), held[:, :, :, rows_v:].reshape(-1, cols)


def on_device(activations, out_grads, v_bank, u_bank, query_ids):
    tok_rows = activations.shape[0]
    queries = query_ids.shape[0]
    n = lax.axis_size(OUTER) * lax.axis_size(MIDDLE) * lax.axis_size(CORE)
    warm = [ring_step(activations[:8, :128], axis) for axis in (OUTER, MIDDLE)]
    both = pick_columns(v_bank, u_bank, query_ids)
    both, warm = lax.optimization_barrier((both, warm))
    v_full, u_full = gather_factors(both, v_bank.shape[0])
    proj_in = folder(activations, v_full)
    proj_out = folder(out_grads, u_full)
    scores = (proj_in * proj_out).reshape(tok_rows, queries, RANK).sum(axis=2)
    total = total_over(jnp.sum(scores * scores, axis=0), TOK, n)
    total = total + 0.0 * sum(w[0, 0].astype(jnp.float32) for w in warm)
    scale = jnp.sqrt(total / (tok_rows * n) + 1e-06)
    return scores / scale[None, :]


def split_mesh(mesh):
    grp, tok = mesh.devices.shape
    assert tok % 8 == 0
    return Mesh(mesh.devices.reshape(grp, tok // 8, 4, 2), ("grp",) + TOK)


def solution(mesh):
    rows = P(TOK, None)
    return jax.shard_map(
        on_device,
        mesh=split_mesh(mesh),
        in_specs=(rows, rows, rows, rows, P("grp")),
        out_specs=P(TOK, "grp"),
        check_vma=False,
    )
```

```python
import jax
import jax.numpy as jnp
from jax import lax
from jax.sharding import Mesh, PartitionSpec as P
from jax.experimental import pallas as pl
from jax.experimental.pallas import tpu as pltpu

RANK = 32
LANES = 128
PER_TILE = LANES // RANK


def pick_kernel(ids_ref, v_ref, u_ref, out, v_buf, u_buf, sems):
    queries = ids_ref.shape[0]
    copies = []
    for k, (bank, buf) in enumerate(((v_ref, v_buf), (u_ref, u_buf))):
        last = bank.shape[1] // LANES - 1
        for q in range(queries):
            tile = jnp.minimum(jnp.maximum(ids_ref[q] // PER_TILE, 0), last)
            start = pl.multiple_of(tile * LANES, LANES)
            copy = pltpu.make_async_copy(bank.at[:, pl.ds(start, LANES)], buf.at[q], sems.at[k, q])
            copy.start()
            copies.append(copy)
    bases = (0, v_buf.shape[1])
    for k, buf in enumerate((v_buf, u_buf)):
        rows = buf.shape[1]
        base = bases[k]
        lane = lax.broadcasted_iota(jnp.int32, (rows, LANES), 1)
        for g in range(queries // PER_TILE):
            acc = jnp.zeros((rows, LANES), buf.dtype)
            for j in range(PER_TILE):
                q = g * PER_TILE + j
                copies[k * queries + q].wait()
                x = buf[q]
                off = (ids_ref[q] % PER_TILE) * RANK
                shift = (RANK * j - off + LANES) % LANES
                moved = pltpu.roll(x, shift, 1)
                keep = (lane >= RANK * j) & (lane < RANK * (j + 1))
                acc = jnp.where(keep, moved, acc)
            out[base:base + rows, g * LANES:(g + 1) * LANES] = acc


def pick_columns(v_bank, u_bank, query_ids):
    queries = query_ids.shape[0]
    assert queries % PER_TILE == 0
    vmem = pl.BlockSpec(memory_space=pltpu.VMEM)
    return pl.pallas_call(
        pick_kernel,
        out_shape=jax.ShapeDtypeStruct((v_bank.shape[0] + u_bank.shape[0], queries * RANK), v_bank.dtype),
        in_specs=[
            pl.BlockSpec(memory_space=pltpu.SMEM),
            pl.BlockSpec(memory_space=pl.ANY),
            pl.BlockSpec(memory_space=pl.ANY),
        ],
        out_specs=vmem,
        scratch_shapes=[
            pltpu.VMEM((queries, v_bank.shape[0], LANES), v_bank.dtype),
            pltpu.VMEM((queries, u_bank.shape[0], LANES), u_bank.dtype),
            pltpu.SemaphoreType.DMA((2, queries)),
        ],
    )(query_ids, v_bank, u_bank)


OUTER = "tok_o"
MIDDLE = "tok_m"
CORE = "tok_c"
TOK = (OUTER, MIDDLE, CORE)


def folder(left, piece):
    return jnp.dot(left, piece, preferred_element_type=jnp.float32)


def total_over(x, axis, n):
    copies = jnp.broadcast_to(x[None], (n,) + x.shape)
    return lax.all_to_all(copies, axis, 0, 0, tiled=False).sum(axis=0)


def spread(x, axis, at):
    k = lax.axis_size(axis)
    copies = jnp.broadcast_to(jnp.expand_dims(x, at), x.shape[:at] + (k,) + x.shape[at:])
    return lax.all_to_all(copies, axis, at, at, tiled=True)


def shifted(x, axis, at):
    k = lax.axis_size(axis)
    if k > 4:
        return spread(x, axis, at)
    me = lax.axis_index(axis)
    got = [x] + [lax.ppermute(x, axis, [(j, (j + s) % k) for j in range(k)]) for s in range(1, k)]
    slots = []
    for o in range(k):
        value = got[0]
        for s in range(1, k):
            value = jnp.where((me - s + k) % k == o, got[s], value)
        slots.append(value)
    return jnp.stack(slots, axis=at)


def gather_factors(both, rows_v):
    cols = both.shape[1]
    held = shifted(both, OUTER, 0)
    held = shifted(held, MIDDLE, 1)
    held = spread(held, CORE, 2)
    return held[:, :, :, :rows_v].reshape(-1, cols), held[:, :, :, rows_v:].reshape(-1, cols)


def on_device(activations, out_grads, v_bank, u_bank, query_ids):
    tok_rows = activations.shape[0]
    queries = query_ids.shape[0]
    n = lax.axis_size(OUTER) * lax.axis_size(MIDDLE) * lax.axis_size(CORE)
    both = pick_columns(v_bank, u_bank, query_ids)
    v_full, u_full = gather_factors(both, v_bank.shape[0])
    proj_in = folder(activations, v_full)
    proj_out = folder(out_grads, u_full)
    scores = (proj_in * proj_out).reshape(tok_rows, queries, RANK).sum(axis=2)
    total = total_over(jnp.sum(scores * scores, axis=0), TOK, n)
    scale = jnp.sqrt(total / (tok_rows * n) + 1e-06)
    return scores / scale[None, :]


def split_mesh(mesh):
    grp, tok = mesh.devices.shape
    assert tok % 8 == 0
    return Mesh(mesh.devices.reshape(grp, tok // 8, 4, 2), ("grp",) + TOK)


def solution(mesh):
    rows = P(TOK, None)
    return jax.shard_map(
        on_device,
        mesh=split_mesh(mesh),
        in_specs=(rows, rows, rows, rows, P("grp")),
        out_specs=P(TOK, "grp"),
        check_vma=False,
    )
```

```python
import jax
import jax.numpy as jnp
from jax import lax
from jax.sharding import Mesh, PartitionSpec as P
from jax.experimental import pallas as pl
from jax.experimental.pallas import tpu as pltpu

RANK = 32
LANES = 128
PER_TILE = LANES // RANK


def pick_kernel(ids_ref, v_ref, u_ref, out, v_buf, u_buf, sems):
    queries = ids_ref.shape[0]
    copies = []
    for k, (bank, buf) in enumerate(((v_ref, v_buf), (u_ref, u_buf))):
        last = bank.shape[1] // LANES - 1
        for q in range(queries):
            tile = jnp.minimum(jnp.maximum(ids_ref[q] // PER_TILE, 0), last)
            start = pl.multiple_of(tile * LANES, LANES)
            copy = pltpu.make_async_copy(bank.at[:, pl.ds(start, LANES)], buf.at[q], sems.at[k, q])
            copy.start()
            copies.append(copy)
    bases = (0, v_buf.shape[1])
    for k, buf in enumerate((v_buf, u_buf)):
        rows = buf.shape[1]
        base = bases[k]
        lane = lax.broadcasted_iota(jnp.int32, (rows, LANES), 1)
        for g in range(queries // PER_TILE):
            acc = jnp.zeros((rows, LANES), buf.dtype)
            for j in range(PER_TILE):
                q = g * PER_TILE + j
                copies[k * queries + q].wait()
                x = buf[q]
                off = (ids_ref[q] % PER_TILE) * RANK
                shift = (RANK * j - off + LANES) % LANES
                moved = pltpu.roll(x, shift, 1)
                keep = (lane >= RANK * j) & (lane < RANK * (j + 1))
                acc = jnp.where(keep, moved, acc)
            out[base:base + rows, g * LANES:(g + 1) * LANES] = acc


def pick_columns(v_bank, u_bank, query_ids):
    queries = query_ids.shape[0]
    assert queries % PER_TILE == 0
    vmem = pl.BlockSpec(memory_space=pltpu.VMEM)
    return pl.pallas_call(
        pick_kernel,
        out_shape=jax.ShapeDtypeStruct((v_bank.shape[0] + u_bank.shape[0], queries * RANK), v_bank.dtype),
        in_specs=[
            pl.BlockSpec(memory_space=pltpu.SMEM),
            pl.BlockSpec(memory_space=pl.ANY),
            pl.BlockSpec(memory_space=pl.ANY),
        ],
        out_specs=vmem,
        scratch_shapes=[
            pltpu.VMEM((queries, v_bank.shape[0], LANES), v_bank.dtype),
            pltpu.VMEM((queries, u_bank.shape[0], LANES), u_bank.dtype),
            pltpu.SemaphoreType.DMA((2, queries)),
        ],
    )(query_ids, v_bank, u_bank)


OUTER = "tok_o"
MIDDLE = "tok_m"
CORE = "tok_c"
TOK = (OUTER, MIDDLE, CORE)


def folder(left, piece):
    return jnp.dot(left, piece, preferred_element_type=jnp.float32)


def total_over(x, axis, n):
    copies = jnp.broadcast_to(x[None], (n,) + x.shape)
    return lax.all_to_all(copies, axis, 0, 0, tiled=False).sum(axis=0)


def spread(x, axis, at):
    k = lax.axis_size(axis)
    copies = jnp.broadcast_to(jnp.expand_dims(x, at), x.shape[:at] + (k,) + x.shape[at:])
    return lax.all_to_all(copies, axis, at, at, tiled=True)


def shifted(x, axis, at):
    k = lax.axis_size(axis)
    if k > 4:
        return spread(x, axis, at)
    me = lax.axis_index(axis)
    got = [x] + [lax.ppermute(x, axis, [(j, (j + s) % k) for j in range(k)]) for s in range(1, k)]
    slots = []
    for o in range(k):
        value = got[0]
        for s in range(1, k):
            value = jnp.where((me - s + k) % k == o, got[s], value)
        slots.append(value)
    return jnp.stack(slots, axis=at)


def gather_factors(both, rows_v):
    cols = both.shape[1]
    held = shifted(both, OUTER, 0)
    held = shifted(held, MIDDLE, 1)
    mine = held
    other = lax.ppermute(held, CORE, [(0, 1), (1, 0)])
    first = lax.axis_index(CORE) == 0
    low = jnp.where(first, mine, other)
    high = jnp.where(first, other, mine)

    def part(lo, hi):
        return jnp.stack([low[:, :, lo:hi], high[:, :, lo:hi]], axis=2).reshape(-1, cols)

    return part(0, rows_v), part(rows_v, both.shape[0])


def on_device(activations, out_grads, v_bank, u_bank, query_ids):
    tok_rows = activations.shape[0]
    queries = query_ids.shape[0]
    n = lax.axis_size(OUTER) * lax.axis_size(MIDDLE) * lax.axis_size(CORE)
    both = pick_columns(v_bank, u_bank, query_ids)
    v_full, u_full = gather_factors(both, v_bank.shape[0])
    proj_in = folder(activations, v_full)
    proj_out = folder(out_grads, u_full)
    scores = (proj_in * proj_out).reshape(tok_rows, queries, RANK).sum(axis=2)
    total = total_over(jnp.sum(scores * scores, axis=0), TOK, n)
    scale = jnp.sqrt(total / (tok_rows * n) + 1e-06)
    return scores / scale[None, :]


def split_mesh(mesh):
    grp, tok = mesh.devices.shape
    assert tok % 8 == 0
    return Mesh(mesh.devices.reshape(grp, tok // 8, 4, 2), ("grp",) + TOK)


def solution(mesh):
    rows = P(TOK, None)
    return jax.shard_map(
        on_device,
        mesh=split_mesh(mesh),
        in_specs=(rows, rows, rows, rows, P("grp")),
        out_specs=P(TOK, "grp"),
        check_vma=False,
    )
```

```python
import jax
import jax.numpy as jnp
from jax import lax
from jax.sharding import Mesh, PartitionSpec as P
from jax.experimental import pallas as pl
from jax.experimental.pallas import tpu as pltpu

RANK = 32
LANES = 128
PER_TILE = LANES // RANK


def pick_kernel(ids_ref, v_ref, u_ref, out, v_buf, u_buf, sems):
    queries = ids_ref.shape[0]
    copies = []
    for k, (bank, buf) in enumerate(((v_ref, v_buf), (u_ref, u_buf))):
        last = bank.shape[1] // LANES - 1
        for q in range(queries):
            tile = jnp.minimum(jnp.maximum(ids_ref[q] // PER_TILE, 0), last)
            start = pl.multiple_of(tile * LANES, LANES)
            copy = pltpu.make_async_copy(bank.at[:, pl.ds(start, LANES)], buf.at[q], sems.at[k, q])
            copy.start()
            copies.append(copy)
    bases = (0, v_buf.shape[1])
    for k, buf in enumerate((v_buf, u_buf)):
        rows = buf.shape[1]
        base = bases[k]
        lane = lax.broadcasted_iota(jnp.int32, (rows, LANES), 1)
        for g in range(queries // PER_TILE):
            acc = jnp.zeros((rows, LANES), buf.dtype)
            for j in range(PER_TILE):
                q = g * PER_TILE + j
                copies[k * queries + q].wait()
                x = buf[q]
                off = (ids_ref[q] % PER_TILE) * RANK
                shift = (RANK * j - off + LANES) % LANES
                moved = pltpu.roll(x, shift, 1)
                keep = (lane >= RANK * j) & (lane < RANK * (j + 1))
                acc = jnp.where(keep, moved, acc)
            out[base:base + rows, g * LANES:(g + 1) * LANES] = acc


def pick_columns(v_bank, u_bank, query_ids):
    queries = query_ids.shape[0]
    assert queries % PER_TILE == 0
    vmem = pl.BlockSpec(memory_space=pltpu.VMEM)
    return pl.pallas_call(
        pick_kernel,
        out_shape=jax.ShapeDtypeStruct((v_bank.shape[0] + u_bank.shape[0], queries * RANK), v_bank.dtype),
        in_specs=[
            pl.BlockSpec(memory_space=pltpu.SMEM),
            pl.BlockSpec(memory_space=pl.ANY),
            pl.BlockSpec(memory_space=pl.ANY),
        ],
        out_specs=vmem,
        scratch_shapes=[
            pltpu.VMEM((queries, v_bank.shape[0], LANES), v_bank.dtype),
            pltpu.VMEM((queries, u_bank.shape[0], LANES), u_bank.dtype),
            pltpu.SemaphoreType.DMA((2, queries)),
        ],
    )(query_ids, v_bank, u_bank)


OUTER = "tok_o"
MIDDLE = "tok_m"
CORE = "tok_c"
TOK = (OUTER, MIDDLE, CORE)


def folder(left, piece):
    return jnp.dot(left, piece, preferred_element_type=jnp.float32)


def total_over(x, axis, n):
    copies = jnp.broadcast_to(x[None], (n,) + x.shape)
    return lax.all_to_all(copies, axis, 0, 0, tiled=False).sum(axis=0)


def spread(x, axis, at):
    k = lax.axis_size(axis)
    copies = jnp.broadcast_to(jnp.expand_dims(x, at), x.shape[:at] + (k,) + x.shape[at:])
    return lax.all_to_all(copies, axis, at, at, tiled=True)


def shifted(x, axis, at):
    k = lax.axis_size(axis)
    if k > 4:
        return spread(x, axis, at)
    me = lax.axis_index(axis)
    got = [x] + [lax.ppermute(x, axis, [(j, (j + s) % k) for j in range(k)]) for s in range(1, k)]
    slots = []
    for o in range(k):
        value = got[0]
        for s in range(1, k):
            value = jnp.where((me - s + k) % k == o, got[s], value)
        slots.append(value)
    return jnp.stack(slots, axis=at)


def gather_factors(both, rows_v):
    cols = both.shape[1]
    held = shifted(both, OUTER, 0)
    held = shifted(held, MIDDLE, 1)
    v_full = spread(held[:, :, :rows_v], CORE, 2)
    u_full = spread(held[:, :, rows_v:], CORE, 2)
    return v_full.reshape(-1, cols), u_full.reshape(-1, cols)


def on_device(activations, out_grads, v_bank, u_bank, query_ids):
    tok_rows = activations.shape[0]
    queries = query_ids.shape[0]
    n = lax.axis_size(OUTER) * lax.axis_size(MIDDLE) * lax.axis_size(CORE)
    both = pick_columns(v_bank, u_bank, query_ids)
    v_full, u_full = gather_factors(both, v_bank.shape[0])
    proj_in = folder(activations, v_full)
    proj_out = folder(out_grads, u_full)
    scores = (proj_in * proj_out).reshape(tok_rows, queries, RANK).sum(axis=2)
    total = total_over(jnp.sum(scores * scores, axis=0), TOK, n)
    scale = jnp.sqrt(total / (tok_rows * n) + 1e-06)
    return scores / scale[None, :]


def split_mesh(mesh):
    grp, tok = mesh.devices.shape
    assert tok % 8 == 0
    return Mesh(mesh.devices.reshape(grp, tok // 8, 4, 2), ("grp",) + TOK)


def solution(mesh):
    rows = P(TOK, None)
    return jax.shard_map(
        on_device,
        mesh=split_mesh(mesh),
        in_specs=(rows, rows, rows, rows, P("grp")),
        out_specs=P(TOK, "grp"),
        check_vma=False,
    )
```

```python
import jax
import jax.numpy as jnp
from jax import lax
from jax.sharding import Mesh, PartitionSpec as P
from jax.experimental import pallas as pl
from jax.experimental.pallas import tpu as pltpu

RANK = 32
LANES = 128
PER_TILE = LANES // RANK


def pick_kernel(ids_ref, v_ref, u_ref, out, v_buf, u_buf, sems):
    queries = ids_ref.shape[0]
    copies = []
    for k, (bank, buf) in enumerate(((v_ref, v_buf), (u_ref, u_buf))):
        last = bank.shape[1] // LANES - 1
        for q in range(queries):
            tile = jnp.minimum(jnp.maximum(ids_ref[q] // PER_TILE, 0), last)
            start = pl.multiple_of(tile * LANES, LANES)
            copy = pltpu.make_async_copy(bank.at[:, pl.ds(start, LANES)], buf.at[q], sems.at[k, q])
            copy.start()
            copies.append(copy)
    bases = (0, v_buf.shape[1])
    for k, buf in enumerate((v_buf, u_buf)):
        rows = buf.shape[1]
        base = bases[k]
        lane = lax.broadcasted_iota(jnp.int32, (rows, LANES), 1)
        for g in range(queries // PER_TILE):
            acc = jnp.zeros((rows, LANES), buf.dtype)
            for j in range(PER_TILE):
                q = g * PER_TILE + j
                copies[k * queries + q].wait()
                x = buf[q]
                off = (ids_ref[q] % PER_TILE) * RANK
                shift = (RANK * j - off + LANES) % LANES
                moved = pltpu.roll(x, shift, 1)
                keep = (lane >= RANK * j) & (lane < RANK * (j + 1))
                acc = jnp.where(keep, moved, acc)
            out[base:base + rows, g * LANES:(g + 1) * LANES] = acc


def pick_columns(v_bank, u_bank, query_ids):
    queries = query_ids.shape[0]
    assert queries % PER_TILE == 0
    vmem = pl.BlockSpec(memory_space=pltpu.VMEM)
    return pl.pallas_call(
        pick_kernel,
        out_shape=jax.ShapeDtypeStruct((v_bank.shape[0] + u_bank.shape[0], queries * RANK), v_bank.dtype),
        in_specs=[
            pl.BlockSpec(memory_space=pltpu.SMEM),
            pl.BlockSpec(memory_space=pl.ANY),
            pl.BlockSpec(memory_space=pl.ANY),
        ],
        out_specs=vmem,
        scratch_shapes=[
            pltpu.VMEM((queries, v_bank.shape[0], LANES), v_bank.dtype),
            pltpu.VMEM((queries, u_bank.shape[0], LANES), u_bank.dtype),
            pltpu.SemaphoreType.DMA((2, queries)),
        ],
    )(query_ids, v_bank, u_bank)


OUTER = "tok_o"
MIDDLE = "tok_m"
CORE = "tok_c"
TOK = (OUTER, MIDDLE, CORE)


def folder(left, piece):
    return jnp.dot(left, piece, preferred_element_type=jnp.float32)


def total_over(x, axis, n):
    copies = jnp.broadcast_to(x[None], (n,) + x.shape)
    return lax.all_to_all(copies, axis, 0, 0, tiled=False).sum(axis=0)


def spread(x, axis, at):
    k = lax.axis_size(axis)
    copies = jnp.broadcast_to(jnp.expand_dims(x, at), x.shape[:at] + (k,) + x.shape[at:])
    return lax.all_to_all(copies, axis, at, at, tiled=True)


def shifted(x, axis, at):
    k = lax.axis_size(axis)
    if k > 4:
        return spread(x, axis, at)
    me = lax.axis_index(axis)
    got = [x] + [lax.ppermute(x, axis, [(j, (j + s) % k) for j in range(k)]) for s in range(1, k)]
    slots = []
    for o in range(k):
        value = got[0]
        for s in range(1, k):
            value = jnp.where((me - s + k) % k == o, got[s], value)
        slots.append(value)
    return jnp.stack(slots, axis=at)


def gather_factors(both, rows_v):
    cols = both.shape[1]
    held = shifted(both, OUTER, 0)
    held = shifted(held, MIDDLE, 1)
    held = spread(held, CORE, 2)
    return held[:, :, :, :rows_v].reshape(-1, cols), held[:, :, :, rows_v:].reshape(-1, cols)


def on_device(activations, out_grads, v_bank, u_bank, query_ids):
    tok_rows = activations.shape[0]
    queries = query_ids.shape[0]
    n = lax.axis_size(OUTER) * lax.axis_size(MIDDLE) * lax.axis_size(CORE)
    both = pick_columns(v_bank, u_bank, query_ids)
    v_full, u_full = gather_factors(both, v_bank.shape[0])
    proj_in = folder(activations, v_full)
    proj_out = folder(out_grads, u_full)
    scores = (proj_in * proj_out).reshape(tok_rows, queries, RANK).sum(axis=2)
    part = jnp.sum(scores * scores, axis=0)
    part = part + lax.ppermute(part, CORE, [(0, 1), (1, 0)])
    total = total_over(part, (OUTER, MIDDLE), n // lax.axis_size(CORE))
    scale = jnp.sqrt(total / (tok_rows * n) + 1e-06)
    return scores / scale[None, :]


def split_mesh(mesh):
    grp, tok = mesh.devices.shape
    assert tok % 8 == 0
    return Mesh(mesh.devices.reshape(grp, tok // 8, 4, 2), ("grp",) + TOK)


def solution(mesh):
    rows = P(TOK, None)
    return jax.shard_map(
        on_device,
        mesh=split_mesh(mesh),
        in_specs=(rows, rows, rows, rows, P("grp")),
        out_specs=P(TOK, "grp"),
        check_vma=False,
    )
```

```python
import jax
import jax.numpy as jnp
from jax import lax
from jax.sharding import Mesh, PartitionSpec as P
from jax.experimental import pallas as pl
from jax.experimental.pallas import tpu as pltpu

RANK = 32
LANES = 128
PER_TILE = LANES // RANK


def pick_kernel(ids_ref, v_ref, u_ref, out, v_buf, u_buf, sems):
    queries = ids_ref.shape[0]
    copies = []
    for k, (bank, buf) in enumerate(((v_ref, v_buf), (u_ref, u_buf))):
        last = bank.shape[1] // LANES - 1
        for q in range(queries):
            tile = jnp.minimum(jnp.maximum(ids_ref[q] // PER_TILE, 0), last)
            start = pl.multiple_of(tile * LANES, LANES)
            copy = pltpu.make_async_copy(bank.at[:, pl.ds(start, LANES)], buf.at[q], sems.at[k, q])
            copy.start()
            copies.append(copy)
    bases = (0, v_buf.shape[1])
    for k, buf in enumerate((v_buf, u_buf)):
        rows = buf.shape[1]
        base = bases[k]
        lane = lax.broadcasted_iota(jnp.int32, (rows, LANES), 1)
        for g in range(queries // PER_TILE):
            acc = jnp.zeros((rows, LANES), buf.dtype)
            for j in range(PER_TILE):
                q = g * PER_TILE + j
                copies[k * queries + q].wait()
                x = buf[q]
                off = (ids_ref[q] % PER_TILE) * RANK
                shift = (RANK * j - off + LANES) % LANES
                moved = pltpu.roll(x, shift, 1)
                keep = (lane >= RANK * j) & (lane < RANK * (j + 1))
                acc = jnp.where(keep, moved, acc)
            out[base:base + rows, g * LANES:(g + 1) * LANES] = acc


def pick_columns(v_bank, u_bank, query_ids):
    queries = query_ids.shape[0]
    assert queries % PER_TILE == 0
    vmem = pl.BlockSpec(memory_space=pltpu.VMEM)
    return pl.pallas_call(
        pick_kernel,
        out_shape=jax.ShapeDtypeStruct((v_bank.shape[0] + u_bank.shape[0], queries * RANK), v_bank.dtype),
        in_specs=[
            pl.BlockSpec(memory_space=pltpu.SMEM),
            pl.BlockSpec(memory_space=pl.ANY),
            pl.BlockSpec(memory_space=pl.ANY),
        ],
        out_specs=vmem,
        scratch_shapes=[
            pltpu.VMEM((queries, v_bank.shape[0], LANES), v_bank.dtype),
            pltpu.VMEM((queries, u_bank.shape[0], LANES), u_bank.dtype),
            pltpu.SemaphoreType.DMA((2, queries)),
        ],
    )(query_ids, v_bank, u_bank)


OUTER = "tok_o"
MIDDLE = "tok_m"
CORE = "tok_c"
TOK = (OUTER, MIDDLE, CORE)


def folder(left, piece):
    return jnp.dot(left, piece, preferred_element_type=jnp.float32)


def total_over(x, axis, n):
    copies = jnp.broadcast_to(x[None], (n,) + x.shape)
    return lax.all_to_all(copies, axis, 0, 0, tiled=False).sum(axis=0)


def spread(x, axis, at):
    k = lax.axis_size(axis)
    copies = jnp.broadcast_to(jnp.expand_dims(x, at), x.shape[:at] + (k,) + x.shape[at:])
    return lax.all_to_all(copies, axis, at, at, tiled=True)


def shifted(x, axis, at):
    k = lax.axis_size(axis)
    if k > 4:
        return spread(x, axis, at)
    me = lax.axis_index(axis)
    got = [x] + [lax.ppermute(x, axis, [(j, (j + s) % k) for j in range(k)]) for s in range(1, k)]
    slots = []
    for o in range(k):
        value = got[0]
        for s in range(1, k):
            value = jnp.where((me - s + k) % k == o, got[s], value)
        slots.append(value)
    return jnp.stack(slots, axis=at)


def halves(x, rows, first):
    tok_rows = x.shape[0]
    grouped = x.reshape(tok_rows, -1, 2, rows)
    own = jnp.where(first, grouped[:, :, 0], grouped[:, :, 1])
    other = jnp.where(first, grouped[:, :, 1], grouped[:, :, 0])
    return own.reshape(tok_rows, -1), other.reshape(tok_rows, -1)


def on_device(activations, out_grads, v_bank, u_bank, query_ids):
    tok_rows = activations.shape[0]
    queries = query_ids.shape[0]
    rows_v, rows_u = v_bank.shape[0], u_bank.shape[0]
    n = lax.axis_size(OUTER) * lax.axis_size(MIDDLE) * lax.axis_size(CORE)
    first = lax.axis_index(CORE) == 0
    both = pick_columns(v_bank, u_bank, query_ids)
    cols = both.shape[1]
    held = shifted(both, OUTER, 0)
    held = shifted(held, MIDDLE, 1)
    sent = lax.ppermute(held, CORE, [(0, 1), (1, 0)])
    act_own, act_other = halves(activations, rows_v, first)
    grad_own, grad_other = halves(out_grads, rows_u, first)
    proj_in = folder(act_own, held[:, :, :rows_v].reshape(-1, cols))
    proj_out = folder(grad_own, held[:, :, rows_v:].reshape(-1, cols))
    proj_in = proj_in + folder(act_other, sent[:, :, :rows_v].reshape(-1, cols))
    proj_out = proj_out + folder(grad_other, sent[:, :, rows_v:].reshape(-1, cols))
    scores = (proj_in * proj_out).reshape(tok_rows, queries, RANK).sum(axis=2)
    total = total_over(jnp.sum(scores * scores, axis=0), TOK, n)
    scale = jnp.sqrt(total / (tok_rows * n) + 1e-06)
    return scores / scale[None, :]


def split_mesh(mesh):
    grp, tok = mesh.devices.shape
    assert tok % 8 == 0
    return Mesh(mesh.devices.reshape(grp, tok // 8, 4, 2), ("grp",) + TOK)


def solution(mesh):
    rows = P(TOK, None)
    return jax.shard_map(
        on_device,
        mesh=split_mesh(mesh),
        in_specs=(rows, rows, rows, rows, P("grp")),
        out_specs=P(TOK, "grp"),
        check_vma=False,
    )
```

```python
import jax
import jax.numpy as jnp
from jax import lax
from jax.sharding import Mesh, PartitionSpec as P
from jax.experimental import pallas as pl
from jax.experimental.pallas import tpu as pltpu

RANK = 32
LANES = 128
PER_TILE = LANES // RANK


def pick_kernel(ids_ref, v_ref, u_ref, out, v_buf, u_buf, sems):
    queries = ids_ref.shape[0]
    copies = []
    for k, (bank, buf) in enumerate(((v_ref, v_buf), (u_ref, u_buf))):
        last = bank.shape[1] // LANES - 1
        for q in range(queries):
            tile = jnp.minimum(jnp.maximum(ids_ref[q] // PER_TILE, 0), last)
            start = pl.multiple_of(tile * LANES, LANES)
            copy = pltpu.make_async_copy(bank.at[:, pl.ds(start, LANES)], buf.at[q], sems.at[k, q])
            copy.start()
            copies.append(copy)
    bases = (0, v_buf.shape[1])
    for k, buf in enumerate((v_buf, u_buf)):
        rows = buf.shape[1]
        base = bases[k]
        lane = lax.broadcasted_iota(jnp.int32, (rows, LANES), 1)
        for g in range(queries // PER_TILE):
            acc = jnp.zeros((rows, LANES), buf.dtype)
            for j in range(PER_TILE):
                q = g * PER_TILE + j
                copies[k * queries + q].wait()
                x = buf[q]
                off = (ids_ref[q] % PER_TILE) * RANK
                shift = (RANK * j - off + LANES) % LANES
                moved = pltpu.roll(x, shift, 1)
                keep = (lane >= RANK * j) & (lane < RANK * (j + 1))
                acc = jnp.where(keep, moved, acc)
            out[base:base + rows, g * LANES:(g + 1) * LANES] = acc


def pick_columns(v_bank, u_bank, query_ids):
    queries = query_ids.shape[0]
    assert queries % PER_TILE == 0
    vmem = pl.BlockSpec(memory_space=pltpu.VMEM)
    return pl.pallas_call(
        pick_kernel,
        out_shape=jax.ShapeDtypeStruct((v_bank.shape[0] + u_bank.shape[0], queries * RANK), v_bank.dtype),
        in_specs=[
            pl.BlockSpec(memory_space=pltpu.SMEM),
            pl.BlockSpec(memory_space=pl.ANY),
            pl.BlockSpec(memory_space=pl.ANY),
        ],
        out_specs=vmem,
        scratch_shapes=[
            pltpu.VMEM((queries, v_bank.shape[0], LANES), v_bank.dtype),
            pltpu.VMEM((queries, u_bank.shape[0], LANES), u_bank.dtype),
            pltpu.SemaphoreType.DMA((2, queries)),
        ],
    )(query_ids, v_bank, u_bank)


OUTER = "tok_o"
MIDDLE = "tok_m"
CORE = "tok_c"
TOK = (OUTER, MIDDLE, CORE)


def folder(left, piece):
    return jnp.dot(left, piece, preferred_element_type=jnp.float32)


def total_over(x, axis, n):
    copies = jnp.broadcast_to(x[None], (n,) + x.shape)
    return lax.all_to_all(copies, axis, 0, 0, tiled=False).sum(axis=0)


def spread(x, axis, at):
    k = lax.axis_size(axis)
    copies = jnp.broadcast_to(jnp.expand_dims(x, at), x.shape[:at] + (k,) + x.shape[at:])
    return lax.all_to_all(copies, axis, at, at, tiled=True)


def shifted(x, axis, at):
    k = lax.axis_size(axis)
    if k > 4:
        return spread(x, axis, at)
    me = lax.axis_index(axis)
    got = [x] + [lax.ppermute(x, axis, [(j, (j + s) % k) for j in range(k)]) for s in range(1, k)]
    slots = []
    for o in range(k):
        value = got[0]
        for s in range(1, k):
            value = jnp.where((me - s + k) % k == o, got[s], value)
        slots.append(value)
    return jnp.stack(slots, axis=at)


def spread_rows(part, first, mine):
    zero = jnp.zeros_like(part)
    if mine:
        pair = [jnp.where(first, part, zero), jnp.where(first, zero, part)]
    else:
        pair = [jnp.where(first, zero, part), jnp.where(first, part, zero)]
    return jnp.stack(pair, axis=2).reshape(-1, part.shape[-1])


def on_device(activations, out_grads, v_bank, u_bank, query_ids):
    tok_rows = activations.shape[0]
    queries = query_ids.shape[0]
    rows_v, rows_u = v_bank.shape[0], u_bank.shape[0]
    n = lax.axis_size(OUTER) * lax.axis_size(MIDDLE) * lax.axis_size(CORE)
    first = lax.axis_index(CORE) == 0
    both = pick_columns(v_bank, u_bank, query_ids)
    cols = both.shape[1]
    held = shifted(both, OUTER, 0)
    held = shifted(held, MIDDLE, 1)
    sent = lax.ppermute(held, CORE, [(0, 1), (1, 0)])
    proj_in = folder(activations, spread_rows(held[:, :, :rows_v], first, True))
    proj_out = folder(out_grads, spread_rows(held[:, :, rows_v:], first, True))
    proj_in = proj_in + folder(activations, spread_rows(sent[:, :, :rows_v], first, False))
    proj_out = proj_out + folder(out_grads, spread_rows(sent[:, :, rows_v:], first, False))
    scores = (proj_in * proj_out).reshape(tok_rows, queries, RANK).sum(axis=2)
    total = total_over(jnp.sum(scores * scores, axis=0), TOK, n)
    scale = jnp.sqrt(total / (tok_rows * n) + 1e-06)
    return scores / scale[None, :]


def split_mesh(mesh):
    grp, tok = mesh.devices.shape
    assert tok % 8 == 0
    return Mesh(mesh.devices.reshape(grp, tok // 8, 4, 2), ("grp",) + TOK)


def solution(mesh):
    rows = P(TOK, None)
    return jax.shard_map(
        on_device,
        mesh=split_mesh(mesh),
        in_specs=(rows, rows, rows, rows, P("grp")),
        out_specs=P(TOK, "grp"),
        check_vma=False,
    )
```

```python
import jax
import jax.numpy as jnp
from jax import lax
from jax.sharding import Mesh, PartitionSpec as P
from jax.experimental import pallas as pl
from jax.experimental.pallas import tpu as pltpu

RANK = 32
LANES = 128
PER_TILE = LANES // RANK


def pick_kernel(ids_ref, v_ref, u_ref, out_hbm, v_buf, u_buf, sems, out, out_sem):
    queries = ids_ref.shape[0]
    copies = []
    for k, (bank, buf) in enumerate(((v_ref, v_buf), (u_ref, u_buf))):
        last = bank.shape[1] // LANES - 1
        for q in range(queries):
            tile = jnp.minimum(jnp.maximum(ids_ref[q] // PER_TILE, 0), last)
            start = pl.multiple_of(tile * LANES, LANES)
            copy = pltpu.make_async_copy(bank.at[:, pl.ds(start, LANES)], buf.at[q], sems.at[k, q])
            copy.start()
            copies.append(copy)
    bases = (0, v_buf.shape[1])
    for k, buf in enumerate((v_buf, u_buf)):
        rows = buf.shape[1]
        base = bases[k]
        lane = lax.broadcasted_iota(jnp.int32, (rows, LANES), 1)
        for g in range(queries // PER_TILE):
            acc = jnp.zeros((rows, LANES), buf.dtype)
            for j in range(PER_TILE):
                q = g * PER_TILE + j
                copies[k * queries + q].wait()
                x = buf[q]
                off = (ids_ref[q] % PER_TILE) * RANK
                shift = (RANK * j - off + LANES) % LANES
                moved = pltpu.roll(x, shift, 1)
                keep = (lane >= RANK * j) & (lane < RANK * (j + 1))
                acc = jnp.where(keep, moved, acc)
            out[base:base + rows, g * LANES:(g + 1) * LANES] = acc
    done = pltpu.make_async_copy(out, out_hbm, out_sem)
    done.start()
    done.wait()


def pick_columns(v_bank, u_bank, query_ids):
    queries = query_ids.shape[0]
    assert queries % PER_TILE == 0
    vmem = pl.BlockSpec(memory_space=pltpu.VMEM)
    return pl.pallas_call(
        pick_kernel,
        out_shape=jax.ShapeDtypeStruct((v_bank.shape[0] + u_bank.shape[0], queries * RANK), v_bank.dtype),
        in_specs=[
            pl.BlockSpec(memory_space=pltpu.SMEM),
            pl.BlockSpec(memory_space=pl.ANY),
            pl.BlockSpec(memory_space=pl.ANY),
        ],
        out_specs=pl.BlockSpec(memory_space=pl.ANY),
        scratch_shapes=[
            pltpu.VMEM((queries, v_bank.shape[0], LANES), v_bank.dtype),
            pltpu.VMEM((queries, u_bank.shape[0], LANES), u_bank.dtype),
            pltpu.SemaphoreType.DMA((2, queries)),
            pltpu.VMEM((v_bank.shape[0] + u_bank.shape[0], queries * RANK), v_bank.dtype),
            pltpu.SemaphoreType.DMA(()),
        ],
    )(query_ids, v_bank, u_bank)


OUTER = "tok_o"
MIDDLE = "tok_m"
CORE = "tok_c"
TOK = (OUTER, MIDDLE, CORE)


def folder(left, piece):
    return jnp.dot(left, piece, preferred_element_type=jnp.float32)


def total_over(x, axis, n):
    copies = jnp.broadcast_to(x[None], (n,) + x.shape)
    return lax.all_to_all(copies, axis, 0, 0, tiled=False).sum(axis=0)


def spread(x, axis, at):
    k = lax.axis_size(axis)
    copies = jnp.broadcast_to(jnp.expand_dims(x, at), x.shape[:at] + (k,) + x.shape[at:])
    return lax.all_to_all(copies, axis, at, at, tiled=True)


def shifted(x, axis, at):
    k = lax.axis_size(axis)
    if k > 4:
        return spread(x, axis, at)
    me = lax.axis_index(axis)
    got = [x] + [lax.ppermute(x, axis, [(j, (j + s) % k) for j in range(k)]) for s in range(1, k)]
    slots = []
    for o in range(k):
        value = got[0]
        for s in range(1, k):
            value = jnp.where((me - s + k) % k == o, got[s], value)
        slots.append(value)
    return jnp.stack(slots, axis=at)


def gather_factors(both, rows_v):
    cols = both.shape[1]
    held = shifted(both, OUTER, 0)
    held = shifted(held, MIDDLE, 1)
    held = spread(held, CORE, 2)
    return held[:, :, :, :rows_v].reshape(-1, cols), held[:, :, :, rows_v:].reshape(-1, cols)


def on_device(activations, out_grads, v_bank, u_bank, query_ids):
    tok_rows = activations.shape[0]
    queries = query_ids.shape[0]
    n = lax.axis_size(OUTER) * lax.axis_size(MIDDLE) * lax.axis_size(CORE)
    both = pick_columns(v_bank, u_bank, query_ids)
    v_full, u_full = gather_factors(both, v_bank.shape[0])
    proj_in = folder(activations, v_full)
    proj_out = folder(out_grads, u_full)
    scores = (proj_in * proj_out).reshape(tok_rows, queries, RANK).sum(axis=2)
    total = total_over(jnp.sum(scores * scores, axis=0), TOK, n)
    scale = jnp.sqrt(total / (tok_rows * n) + 1e-06)
    return scores / scale[None, :]


def split_mesh(mesh):
    grp, tok = mesh.devices.shape
    assert tok % 8 == 0
    return Mesh(mesh.devices.reshape(grp, tok // 8, 4, 2), ("grp",) + TOK)


def solution(mesh):
    rows = P(TOK, None)
    return jax.shard_map(
        on_device,
        mesh=split_mesh(mesh),
        in_specs=(rows, rows, rows, rows, P("grp")),
        out_specs=P(TOK, "grp"),
        check_vma=False,
    )
```

```python
import jax
import jax.numpy as jnp
from jax import lax
from jax.sharding import Mesh, PartitionSpec as P
from jax.experimental import pallas as pl
from jax.experimental.pallas import tpu as pltpu

RANK = 32
LANES = 128
PER_TILE = LANES // RANK


def pick_kernel(ids_ref, v_ref, u_ref, out, v_buf, u_buf, sems):
    queries = ids_ref.shape[0]
    copies = []
    for k, (bank, buf) in enumerate(((v_ref, v_buf), (u_ref, u_buf))):
        last = bank.shape[1] // LANES - 1
        for q in range(queries):
            tile = jnp.minimum(jnp.maximum(ids_ref[q] // PER_TILE, 0), last)
            start = pl.multiple_of(tile * LANES, LANES)
            copy = pltpu.make_async_copy(bank.at[:, pl.ds(start, LANES)], buf.at[q], sems.at[k, q])
            copy.start()
            copies.append(copy)
    bases = (0, v_buf.shape[1])
    for k, buf in enumerate((v_buf, u_buf)):
        rows = buf.shape[1]
        base = bases[k]
        lane = lax.broadcasted_iota(jnp.int32, (rows, LANES), 1)
        for g in range(queries // PER_TILE):
            acc = jnp.zeros((rows, LANES), buf.dtype)
            for j in range(PER_TILE):
                q = g * PER_TILE + j
                copies[k * queries + q].wait()
                x = buf[q]
                off = (ids_ref[q] % PER_TILE) * RANK
                shift = (RANK * j - off + LANES) % LANES
                moved = pltpu.roll(x, shift, 1)
                keep = (lane >= RANK * j) & (lane < RANK * (j + 1))
                acc = jnp.where(keep, moved, acc)
            out[base:base + rows, g * LANES:(g + 1) * LANES] = acc


def pick_columns(v_bank, u_bank, query_ids):
    queries = query_ids.shape[0]
    assert queries % PER_TILE == 0
    vmem = pl.BlockSpec(memory_space=pltpu.VMEM)
    return pl.pallas_call(
        pick_kernel,
        out_shape=jax.ShapeDtypeStruct((v_bank.shape[0] + u_bank.shape[0], queries * RANK), v_bank.dtype),
        in_specs=[
            pl.BlockSpec(memory_space=pltpu.SMEM),
            pl.BlockSpec(memory_space=pl.ANY),
            pl.BlockSpec(memory_space=pl.ANY),
        ],
        out_specs=vmem,
        scratch_shapes=[
            pltpu.VMEM((queries, v_bank.shape[0], LANES), v_bank.dtype),
            pltpu.VMEM((queries, u_bank.shape[0], LANES), u_bank.dtype),
            pltpu.SemaphoreType.DMA((2, queries)),
        ],
    )(query_ids, v_bank, u_bank)


OUTER = "tok_o"
MIDDLE = "tok_m"
CORE = "tok_c"
TOK = (OUTER, MIDDLE, CORE)


def folder(left, piece):
    return jnp.dot(left, piece, preferred_element_type=jnp.float32)


def total_over(x, axis, n):
    copies = jnp.broadcast_to(x[None], (n,) + x.shape)
    return lax.all_to_all(copies, axis, 0, 0, tiled=False).sum(axis=0)


def spread(x, axis, at):
    k = lax.axis_size(axis)
    copies = jnp.broadcast_to(jnp.expand_dims(x, at), x.shape[:at] + (k,) + x.shape[at:])
    return lax.all_to_all(copies, axis, at, at, tiled=True)


def shifted(x, axis, at):
    k = lax.axis_size(axis)
    if k > 4 or k & (k - 1):
        return spread(x, axis, at)
    me = lax.axis_index(axis)
    got = [x] + [lax.ppermute(x, axis, [(j, j ^ s) for j in range(k)]) for s in range(1, k)]
    slots = []
    for o in range(k):
        value = got[0]
        for s in range(1, k):
            value = jnp.where(jnp.bitwise_xor(me, s) == o, got[s], value)
        slots.append(value)
    return jnp.stack(slots, axis=at)


def gather_factors(both, rows_v):
    cols = both.shape[1]
    held = shifted(both, OUTER, 0)
    held = shifted(held, MIDDLE, 1)
    held = spread(held, CORE, 2)
    return held[:, :, :, :rows_v].reshape(-1, cols), held[:, :, :, rows_v:].reshape(-1, cols)


def on_device(activations, out_grads, v_bank, u_bank, query_ids):
    tok_rows = activations.shape[0]
    queries = query_ids.shape[0]
    n = lax.axis_size(OUTER) * lax.axis_size(MIDDLE) * lax.axis_size(CORE)
    both = pick_columns(v_bank, u_bank, query_ids)
    v_full, u_full = gather_factors(both, v_bank.shape[0])
    proj_in = folder(activations, v_full)
    proj_out = folder(out_grads, u_full)
    scores = (proj_in * proj_out).reshape(tok_rows, queries, RANK).sum(axis=2)
    total = total_over(jnp.sum(scores * scores, axis=0), TOK, n)
    scale = jnp.sqrt(total / (tok_rows * n) + 1e-06)
    return scores / scale[None, :]


def split_mesh(mesh):
    grp, tok = mesh.devices.shape
    assert tok % 8 == 0
    return Mesh(mesh.devices.reshape(grp, tok // 8, 4, 2), ("grp",) + TOK)


def solution(mesh):
    rows = P(TOK, None)
    return jax.shard_map(
        on_device,
        mesh=split_mesh(mesh),
        in_specs=(rows, rows, rows, rows, P("grp")),
        out_specs=P(TOK, "grp"),
        check_vma=False,
    )
```

```python
import jax
import jax.numpy as jnp
from jax import lax
from jax.sharding import Mesh, PartitionSpec as P
from jax.experimental import pallas as pl
from jax.experimental.pallas import tpu as pltpu

RANK = 32
LANES = 128
PER_TILE = LANES // RANK


def pick_kernel(ids_ref, v_ref, u_ref, out, v_buf, u_buf, sems):
    queries = ids_ref.shape[0]
    copies = []
    for k, (bank, buf) in enumerate(((v_ref, v_buf), (u_ref, u_buf))):
        last = bank.shape[1] // LANES - 1
        for q in range(queries):
            tile = jnp.minimum(jnp.maximum(ids_ref[q] // PER_TILE, 0), last)
            start = pl.multiple_of(tile * LANES, LANES)
            copy = pltpu.make_async_copy(bank.at[:, pl.ds(start, LANES)], buf.at[q], sems.at[k, q])
            copy.start()
            copies.append(copy)
    for copy in copies:
        copy.wait()
    bases = (0, v_buf.shape[1])
    for k, buf in enumerate((v_buf, u_buf)):
        rows = buf.shape[1]
        base = bases[k]
        lane = lax.broadcasted_iota(jnp.int32, (rows, LANES), 1)
        for g in range(queries // PER_TILE):
            acc = jnp.zeros((rows, LANES), buf.dtype)
            for j in range(PER_TILE):
                q = g * PER_TILE + j
                x = buf[q]
                off = (ids_ref[q] % PER_TILE) * RANK
                shift = (RANK * j - off + LANES) % LANES
                moved = pltpu.roll(x, shift, 1)
                keep = (lane >= RANK * j) & (lane < RANK * (j + 1))
                acc = jnp.where(keep, moved, acc)
            out[base:base + rows, g * LANES:(g + 1) * LANES] = acc


def pick_columns(v_bank, u_bank, query_ids):
    queries = query_ids.shape[0]
    assert queries % PER_TILE == 0
    vmem = pl.BlockSpec(memory_space=pltpu.VMEM)
    return pl.pallas_call(
        pick_kernel,
        out_shape=jax.ShapeDtypeStruct((v_bank.shape[0] + u_bank.shape[0], queries * RANK), v_bank.dtype),
        in_specs=[
            pl.BlockSpec(memory_space=pltpu.SMEM),
            pl.BlockSpec(memory_space=pl.ANY),
            pl.BlockSpec(memory_space=pl.ANY),
        ],
        out_specs=vmem,
        scratch_shapes=[
            pltpu.VMEM((queries, v_bank.shape[0], LANES), v_bank.dtype),
            pltpu.VMEM((queries, u_bank.shape[0], LANES), u_bank.dtype),
            pltpu.SemaphoreType.DMA((2, queries)),
        ],
    )(query_ids, v_bank, u_bank)


OUTER = "tok_o"
MIDDLE = "tok_m"
CORE = "tok_c"
TOK = (OUTER, MIDDLE, CORE)


def folder(left, piece):
    return jnp.dot(left, piece, preferred_element_type=jnp.float32)


def total_over(x, axis, n):
    copies = jnp.broadcast_to(x[None], (n,) + x.shape)
    return lax.all_to_all(copies, axis, 0, 0, tiled=False).sum(axis=0)


def spread(x, axis, at):
    k = lax.axis_size(axis)
    copies = jnp.broadcast_to(jnp.expand_dims(x, at), x.shape[:at] + (k,) + x.shape[at:])
    return lax.all_to_all(copies, axis, at, at, tiled=True)


def shifted(x, axis, at):
    k = lax.axis_size(axis)
    if k > 4 or k & (k - 1):
        return spread(x, axis, at)
    me = lax.axis_index(axis)
    got = [x] + [lax.ppermute(x, axis, [(j, j ^ s) for j in range(k)]) for s in range(1, k)]
    slots = []
    for o in range(k):
        value = got[0]
        for s in range(1, k):
            value = jnp.where(jnp.bitwise_xor(me, s) == o, got[s], value)
        slots.append(value)
    return jnp.stack(slots, axis=at)


def gather_factors(both, rows_v):
    cols = both.shape[1]
    held = shifted(both, OUTER, 0)
    held = shifted(held, MIDDLE, 1)
    held = spread(held, CORE, 2)
    return held[:, :, :, :rows_v].reshape(-1, cols), held[:, :, :, rows_v:].reshape(-1, cols)


def on_device(activations, out_grads, v_bank, u_bank, query_ids):
    tok_rows = activations.shape[0]
    queries = query_ids.shape[0]
    n = lax.axis_size(OUTER) * lax.axis_size(MIDDLE) * lax.axis_size(CORE)
    both = pick_columns(v_bank, u_bank, query_ids)
    v_full, u_full = gather_factors(both, v_bank.shape[0])
    proj_in = folder(activations, v_full)
    proj_out = folder(out_grads, u_full)
    scores = (proj_in * proj_out).reshape(tok_rows, queries, RANK).sum(axis=2)
    total = total_over(jnp.sum(scores * scores, axis=0), TOK, n)
    scale = jnp.sqrt(total / (tok_rows * n) + 1e-06)
    return scores / scale[None, :]


def split_mesh(mesh):
    grp, tok = mesh.devices.shape
    assert tok % 8 == 0
    return Mesh(mesh.devices.reshape(grp, tok // 8, 4, 2), ("grp",) + TOK)


def solution(mesh):
    rows = P(TOK, None)
    return jax.shard_map(
        on_device,
        mesh=split_mesh(mesh),
        in_specs=(rows, rows, rows, rows, P("grp")),
        out_specs=P(TOK, "grp"),
        check_vma=False,
    )
```

```python
import jax
import jax.numpy as jnp
from jax import lax
from jax.sharding import Mesh, PartitionSpec as P
from jax.experimental import pallas as pl
from jax.experimental.pallas import tpu as pltpu

RANK = 32
LANES = 128
PER_TILE = LANES // RANK


def pick_kernel(ids_ref, v_ref, u_ref, out, v_buf, u_buf, sems):
    queries = ids_ref.shape[0]
    copies = []
    for k, (bank, buf) in enumerate(((v_ref, v_buf), (u_ref, u_buf))):
        last = bank.shape[1] // LANES - 1
        for q in range(queries):
            tile = jnp.minimum(jnp.maximum(ids_ref[q] // PER_TILE, 0), last)
            start = pl.multiple_of(tile * LANES, LANES)
            copy = pltpu.make_async_copy(bank.at[:, pl.ds(start, LANES)], buf.at[q], sems.at[k, q])
            copy.start()
            copies.append(copy)
    for copy in copies:
        copy.wait()
    bases = (0, v_buf.shape[1])
    for k, buf in enumerate((v_buf, u_buf)):
        rows = buf.shape[1]
        base = bases[k]
        lane = lax.broadcasted_iota(jnp.int32, (rows, LANES), 1)
        for g in range(queries // PER_TILE):
            acc = jnp.zeros((rows, LANES), buf.dtype)
            for j in range(PER_TILE):
                q = g * PER_TILE + j
                x = buf[q]
                off = (ids_ref[q] % PER_TILE) * RANK
                shift = (RANK * j - off + LANES) % LANES
                moved = pltpu.roll(x, shift, 1)
                keep = (lane >= RANK * j) & (lane < RANK * (j + 1))
                acc = jnp.where(keep, moved, acc)
            out[base:base + rows, g * LANES:(g + 1) * LANES] = acc


def pick_columns(v_bank, u_bank, query_ids):
    queries = query_ids.shape[0]
    assert queries % PER_TILE == 0
    vmem = pl.BlockSpec(memory_space=pltpu.VMEM)
    return pl.pallas_call(
        pick_kernel,
        out_shape=jax.ShapeDtypeStruct((v_bank.shape[0] + u_bank.shape[0], queries * RANK), v_bank.dtype),
        in_specs=[
            pl.BlockSpec(memory_space=pltpu.SMEM),
            pl.BlockSpec(memory_space=pl.ANY),
            pl.BlockSpec(memory_space=pl.ANY),
        ],
        out_specs=vmem,
        scratch_shapes=[
            pltpu.VMEM((queries, v_bank.shape[0], LANES), v_bank.dtype),
            pltpu.VMEM((queries, u_bank.shape[0], LANES), u_bank.dtype),
            pltpu.SemaphoreType.DMA((2, queries)),
        ],
    )(query_ids, v_bank, u_bank)


OUTER = "tok_o"
MIDDLE = "tok_m"
CORE = "tok_c"
TOK = (OUTER, MIDDLE, CORE)


def folder(left, piece):
    return jnp.dot(left, piece, preferred_element_type=jnp.float32)


def total_over(x, axis, n):
    copies = jnp.broadcast_to(x[None], (n,) + x.shape)
    return lax.all_to_all(copies, axis, 0, 0, tiled=False).sum(axis=0)


def spread(x, axis, at):
    k = lax.axis_size(axis)
    copies = jnp.broadcast_to(jnp.expand_dims(x, at), x.shape[:at] + (k,) + x.shape[at:])
    return lax.all_to_all(copies, axis, at, at, tiled=True)


def shifted(x, axis, at):
    k = lax.axis_size(axis)
    if k > 4 or k & (k - 1):
        return spread(x, axis, at)
    me = lax.axis_index(axis)
    got = [x] + [lax.ppermute(x, axis, [(j, j ^ s) for j in range(k)]) for s in range(1, k)]
    by_partner = jnp.stack(got, axis=at)
    order = jnp.bitwise_xor(me, jnp.arange(k, dtype=me.dtype))
    return jnp.take(by_partner, order, axis=at, mode="clip")


def gather_factors(both, rows_v):
    cols = both.shape[1]
    held = shifted(both, OUTER, 0)
    held = shifted(held, MIDDLE, 1)
    held = spread(held, CORE, 2)
    return held[:, :, :, :rows_v].reshape(-1, cols), held[:, :, :, rows_v:].reshape(-1, cols)


def on_device(activations, out_grads, v_bank, u_bank, query_ids):
    tok_rows = activations.shape[0]
    queries = query_ids.shape[0]
    n = lax.axis_size(OUTER) * lax.axis_size(MIDDLE) * lax.axis_size(CORE)
    both = pick_columns(v_bank, u_bank, query_ids)
    v_full, u_full = gather_factors(both, v_bank.shape[0])
    proj_in = folder(activations, v_full)
    proj_out = folder(out_grads, u_full)
    scores = (proj_in * proj_out).reshape(tok_rows, queries, RANK).sum(axis=2)
    total = total_over(jnp.sum(scores * scores, axis=0), TOK, n)
    scale = jnp.sqrt(total / (tok_rows * n) + 1e-06)
    return scores / scale[None, :]


def split_mesh(mesh):
    grp, tok = mesh.devices.shape
    assert tok % 8 == 0
    return Mesh(mesh.devices.reshape(grp, tok // 8, 4, 2), ("grp",) + TOK)


def solution(mesh):
    rows = P(TOK, None)
    return jax.shard_map(
        on_device,
        mesh=split_mesh(mesh),
        in_specs=(rows, rows, rows, rows, P("grp")),
        out_specs=P(TOK, "grp"),
        check_vma=False,
    )
```

```python
import jax
import jax.numpy as jnp
from jax import lax
from jax.sharding import Mesh, PartitionSpec as P
from jax.experimental import pallas as pl
from jax.experimental.pallas import tpu as pltpu

RANK = 32
LANES = 128
PER_TILE = LANES // RANK


def pick_kernel(ids_ref, v_ref, u_ref, out, v_buf, u_buf, sems):
    queries = ids_ref.shape[0]
    copies = []
    for k, (bank, buf) in enumerate(((v_ref, v_buf), (u_ref, u_buf))):
        last = bank.shape[1] // LANES - 1
        for q in range(queries):
            tile = jnp.minimum(jnp.maximum(ids_ref[q] // PER_TILE, 0), last)
            start = pl.multiple_of(tile * LANES, LANES)
            copy = pltpu.make_async_copy(bank.at[:, pl.ds(start, LANES)], buf.at[q], sems.at[k, q])
            copy.start()
            copies.append(copy)
    for copy in copies:
        copy.wait()
    bases = (u_buf.shape[1], 0)
    for k, buf in enumerate((v_buf, u_buf)):
        rows = buf.shape[1]
        base = bases[k]
        lane = lax.broadcasted_iota(jnp.int32, (rows, LANES), 1)
        for g in range(queries // PER_TILE):
            acc = jnp.zeros((rows, LANES), buf.dtype)
            for j in range(PER_TILE):
                q = g * PER_TILE + j
                x = buf[q]
                off = (ids_ref[q] % PER_TILE) * RANK
                shift = (RANK * j - off + LANES) % LANES
                moved = pltpu.roll(x, shift, 1)
                keep = (lane >= RANK * j) & (lane < RANK * (j + 1))
                acc = jnp.where(keep, moved, acc)
            out[base:base + rows, g * LANES:(g + 1) * LANES] = acc


def pick_columns(v_bank, u_bank, query_ids):
    queries = query_ids.shape[0]
    assert queries % PER_TILE == 0
    vmem = pl.BlockSpec(memory_space=pltpu.VMEM)
    return pl.pallas_call(
        pick_kernel,
        out_shape=jax.ShapeDtypeStruct((v_bank.shape[0] + u_bank.shape[0], queries * RANK), v_bank.dtype),
        in_specs=[
            pl.BlockSpec(memory_space=pltpu.SMEM),
            pl.BlockSpec(memory_space=pl.ANY),
            pl.BlockSpec(memory_space=pl.ANY),
        ],
        out_specs=vmem,
        scratch_shapes=[
            pltpu.VMEM((queries, v_bank.shape[0], LANES), v_bank.dtype),
            pltpu.VMEM((queries, u_bank.shape[0], LANES), u_bank.dtype),
            pltpu.SemaphoreType.DMA((2, queries)),
        ],
    )(query_ids, v_bank, u_bank)


OUTER = "tok_o"
MIDDLE = "tok_m"
CORE = "tok_c"
TOK = (OUTER, MIDDLE, CORE)


def folder(left, piece):
    return jnp.dot(left, piece, preferred_element_type=jnp.float32)


def total_over(x, axis, n):
    copies = jnp.broadcast_to(x[None], (n,) + x.shape)
    return lax.all_to_all(copies, axis, 0, 0, tiled=False).sum(axis=0)


def spread(x, axis, at):
    k = lax.axis_size(axis)
    copies = jnp.broadcast_to(jnp.expand_dims(x, at), x.shape[:at] + (k,) + x.shape[at:])
    return lax.all_to_all(copies, axis, at, at, tiled=True)


def shifted(x, axis, at):
    k = lax.axis_size(axis)
    if k > 4 or k & (k - 1):
        return spread(x, axis, at)
    me = lax.axis_index(axis)
    got = [x] + [lax.ppermute(x, axis, [(j, j ^ s) for j in range(k)]) for s in range(1, k)]
    slots = []
    for o in range(k):
        value = got[0]
        for s in range(1, k):
            value = jnp.where(jnp.bitwise_xor(me, s) == o, got[s], value)
        slots.append(value)
    return jnp.stack(slots, axis=at)


def gather_factors(both, rows_v):
    cols = both.shape[1]
    held = shifted(both, OUTER, 0)
    held = shifted(held, MIDDLE, 1)
    held = spread(held, CORE, 2)
    rows_u = held.shape[3] - rows_v
    return held[:, :, :, rows_u:].reshape(-1, cols), held[:, :, :, :rows_u].reshape(-1, cols)


def on_device(activations, out_grads, v_bank, u_bank, query_ids):
    tok_rows = activations.shape[0]
    queries = query_ids.shape[0]
    n = lax.axis_size(OUTER) * lax.axis_size(MIDDLE) * lax.axis_size(CORE)
    both = pick_columns(v_bank, u_bank, query_ids)
    v_full, u_full = gather_factors(both, v_bank.shape[0])
    proj_in = folder(activations, v_full)
    proj_out = folder(out_grads, u_full)
    scores = (proj_in * proj_out).reshape(tok_rows, queries, RANK).sum(axis=2)
    total = total_over(jnp.sum(scores * scores, axis=0), TOK, n)
    scale = jnp.sqrt(total / (tok_rows * n) + 1e-06)
    return scores / scale[None, :]


def split_mesh(mesh):
    grp, tok = mesh.devices.shape
    assert tok % 8 == 0
    return Mesh(mesh.devices.reshape(grp, tok // 8, 4, 2), ("grp",) + TOK)


def solution(mesh):
    rows = P(TOK, None)
    return jax.shard_map(
        on_device,
        mesh=split_mesh(mesh),
        in_specs=(rows, rows, rows, rows, P("grp")),
        out_specs=P(TOK, "grp"),
        check_vma=False,
    )
```

```python
import jax
import jax.numpy as jnp
from jax import lax
from jax.sharding import Mesh, PartitionSpec as P
from jax.experimental import pallas as pl
from jax.experimental.pallas import tpu as pltpu

RANK = 32
LANES = 128
PER_TILE = LANES // RANK


def pick_kernel(ids_ref, v_ref, u_ref, out, v_buf, u_buf, sems):
    queries = ids_ref.shape[0]
    copies = []
    for k, (bank, buf) in enumerate(((v_ref, v_buf), (u_ref, u_buf))):
        last = bank.shape[1] // LANES - 1
        for q in range(queries):
            tile = jnp.minimum(jnp.maximum(ids_ref[q] // PER_TILE, 0), last)
            start = pl.multiple_of(tile * LANES, LANES)
            copy = pltpu.make_async_copy(bank.at[:, pl.ds(start, LANES)], buf.at[q], sems.at[k, q])
            copy.start()
            copies.append(copy)
    bases = (0, v_buf.shape[1])
    for k, buf in enumerate((v_buf, u_buf)):
        for copy in copies[k * queries:(k + 1) * queries]:
            copy.wait()
        rows = buf.shape[1]
        base = bases[k]
        lane = lax.broadcasted_iota(jnp.int32, (rows, LANES), 1)
        for g in range(queries // PER_TILE):
            acc = jnp.zeros((rows, LANES), buf.dtype)
            for j in range(PER_TILE):
                q = g * PER_TILE + j
                x = buf[q]
                off = (ids_ref[q] % PER_TILE) * RANK
                shift = (RANK * j - off + LANES) % LANES
                moved = pltpu.roll(x, shift, 1)
                keep = (lane >= RANK * j) & (lane < RANK * (j + 1))
                acc = jnp.where(keep, moved, acc)
            out[base:base + rows, g * LANES:(g + 1) * LANES] = acc


def pick_columns(v_bank, u_bank, query_ids):
    queries = query_ids.shape[0]
    assert queries % PER_TILE == 0
    vmem = pl.BlockSpec(memory_space=pltpu.VMEM)
    return pl.pallas_call(
        pick_kernel,
        out_shape=jax.ShapeDtypeStruct((v_bank.shape[0] + u_bank.shape[0], queries * RANK), v_bank.dtype),
        in_specs=[
            pl.BlockSpec(memory_space=pltpu.SMEM),
            pl.BlockSpec(memory_space=pl.ANY),
            pl.BlockSpec(memory_space=pl.ANY),
        ],
        out_specs=vmem,
        scratch_shapes=[
            pltpu.VMEM((queries, v_bank.shape[0], LANES), v_bank.dtype),
            pltpu.VMEM((queries, u_bank.shape[0], LANES), u_bank.dtype),
            pltpu.SemaphoreType.DMA((2, queries)),
        ],
    )(query_ids, v_bank, u_bank)


OUTER = "tok_o"
MIDDLE = "tok_m"
CORE = "tok_c"
TOK = (OUTER, MIDDLE, CORE)


def folder(left, piece):
    return jnp.dot(left, piece, preferred_element_type=jnp.float32)


def total_over(x, axis, n):
    copies = jnp.broadcast_to(x[None], (n,) + x.shape)
    return lax.all_to_all(copies, axis, 0, 0, tiled=False).sum(axis=0)


def spread(x, axis, at):
    k = lax.axis_size(axis)
    copies = jnp.broadcast_to(jnp.expand_dims(x, at), x.shape[:at] + (k,) + x.shape[at:])
    return lax.all_to_all(copies, axis, at, at, tiled=True)


def shifted(x, axis, at):
    k = lax.axis_size(axis)
    if k > 4 or k & (k - 1):
        return spread(x, axis, at)
    me = lax.axis_index(axis)
    got = [x] + [lax.ppermute(x, axis, [(j, j ^ s) for j in range(k)]) for s in range(1, k)]
    slots = []
    for o in range(k):
        value = got[0]
        for s in range(1, k):
            value = jnp.where(jnp.bitwise_xor(me, s) == o, got[s], value)
        slots.append(value)
    return jnp.stack(slots, axis=at)


def gather_factors(both, rows_v):
    cols = both.shape[1]
    held = shifted(both, OUTER, 0)
    held = shifted(held, MIDDLE, 1)
    held = spread(held, CORE, 2)
    return held[:, :, :, :rows_v].reshape(-1, cols), held[:, :, :, rows_v:].reshape(-1, cols)


def on_device(activations, out_grads, v_bank, u_bank, query_ids):
    tok_rows = activations.shape[0]
    queries = query_ids.shape[0]
    n = lax.axis_size(OUTER) * lax.axis_size(MIDDLE) * lax.axis_size(CORE)
    both = pick_columns(v_bank, u_bank, query_ids)
    v_full, u_full = gather_factors(both, v_bank.shape[0])
    proj_in = folder(activations, v_full)
    proj_out = folder(out_grads, u_full)
    scores = (proj_in * proj_out).reshape(tok_rows, queries, RANK).sum(axis=2)
    total = total_over(jnp.sum(scores * scores, axis=0), TOK, n)
    scale = jnp.sqrt(total / (tok_rows * n) + 1e-06)
    return scores / scale[None, :]


def split_mesh(mesh):
    grp, tok = mesh.devices.shape
    assert tok % 8 == 0
    return Mesh(mesh.devices.reshape(grp, tok // 8, 4, 2), ("grp",) + TOK)


def solution(mesh):
    rows = P(TOK, None)
    return jax.shard_map(
        on_device,
        mesh=split_mesh(mesh),
        in_specs=(rows, rows, rows, rows, P("grp")),
        out_specs=P(TOK, "grp"),
        check_vma=False,
    )
```

```python
import jax
import jax.numpy as jnp
from jax import lax
from jax.sharding import Mesh, PartitionSpec as P
from jax.experimental import pallas as pl
from jax.experimental.pallas import tpu as pltpu

RANK = 32
LANES = 128
PER_TILE = LANES // RANK


def pick_kernel(ids_ref, v_ref, u_ref, out, v_buf, u_buf, sems):
    queries = ids_ref.shape[0]
    copies = []
    for k, (bank, buf) in enumerate(((v_ref, v_buf), (u_ref, u_buf))):
        last = bank.shape[1] // LANES - 1
        for q in range(queries):
            tile = jnp.minimum(jnp.maximum(ids_ref[q] // PER_TILE, 0), last)
            start = pl.multiple_of(tile * LANES, LANES)
            copy = pltpu.make_async_copy(bank.at[:, pl.ds(start, LANES)], buf.at[q], sems.at[k, q])
            copy.start()
            copies.append(copy)
    for copy in copies:
        copy.wait()
    bases = (0, v_buf.shape[1])
    for k, buf in enumerate((v_buf, u_buf)):
        rows = buf.shape[1]
        base = bases[k]
        lane = lax.broadcasted_iota(jnp.int32, (rows, LANES), 1)
        for g in range(queries // PER_TILE):
            acc = jnp.zeros((rows, LANES), buf.dtype)
            for j in range(PER_TILE):
                q = g * PER_TILE + j
                x = buf[q]
                off = (ids_ref[q] % PER_TILE) * RANK
                shift = (RANK * j - off + LANES) % LANES
                moved = pltpu.roll(x, shift, 1)
                keep = (lane >= RANK * j) & (lane < RANK * (j + 1))
                acc = jnp.where(keep, moved, acc)
            out[base:base + rows, g * LANES:(g + 1) * LANES] = acc


def pick_columns(v_bank, u_bank, query_ids):
    queries = query_ids.shape[0]
    assert queries % PER_TILE == 0
    vmem = pl.BlockSpec(memory_space=pltpu.VMEM)
    return pl.pallas_call(
        pick_kernel,
        out_shape=jax.ShapeDtypeStruct((v_bank.shape[0] + u_bank.shape[0], queries * RANK), v_bank.dtype),
        in_specs=[
            pl.BlockSpec(memory_space=pltpu.SMEM),
            pl.BlockSpec(memory_space=pl.ANY),
            pl.BlockSpec(memory_space=pl.ANY),
        ],
        out_specs=vmem,
        scratch_shapes=[
            pltpu.VMEM((queries, v_bank.shape[0], LANES), v_bank.dtype),
            pltpu.VMEM((queries, u_bank.shape[0], LANES), u_bank.dtype),
            pltpu.SemaphoreType.DMA((2, queries)),
        ],
    )(query_ids, v_bank, u_bank)


OUTER = "tok_o"
MIDDLE = "tok_m"
CORE = "tok_c"
TOK = (OUTER, MIDDLE, CORE)


def folder(left, piece):
    return jnp.dot(left, piece, preferred_element_type=jnp.float32)


def total_over(x, axis, n):
    copies = jnp.broadcast_to(x[None], (n,) + x.shape)
    return lax.all_to_all(copies, axis, 0, 0, tiled=False).sum(axis=0)


def spread(x, axis, at):
    k = lax.axis_size(axis)
    copies = jnp.broadcast_to(jnp.expand_dims(x, at), x.shape[:at] + (k,) + x.shape[at:])
    return lax.all_to_all(copies, axis, at, at, tiled=True)


def shifted(x, axis, at):
    k = lax.axis_size(axis)
    if k > 4 or k & (k - 1):
        return spread(x, axis, at)
    me = lax.axis_index(axis)
    got = [x] + [lax.ppermute(x, axis, [(j, j ^ s) for j in range(k)]) for s in range(1, k)]
    slots = []
    for o in range(k):
        value = got[0]
        for s in range(1, k):
            value = jnp.where(jnp.bitwise_xor(me, s) == o, got[s], value)
        slots.append(value)
    return jnp.stack(slots, axis=at)


def gather_factors(both, rows_v):
    cols = both.shape[1]
    held = shifted(both, OUTER, 0)
    held = shifted(held, MIDDLE, 1)
    held = spread(held, CORE, 2)
    return held[:, :, :, :rows_v].reshape(-1, cols), held[:, :, :, rows_v:].reshape(-1, cols)


def on_device(activations, out_grads, v_bank, u_bank, query_ids):
    tok_rows = activations.shape[0]
    queries = query_ids.shape[0]
    n = lax.axis_size(OUTER) * lax.axis_size(MIDDLE) * lax.axis_size(CORE)
    both = pick_columns(v_bank, u_bank, query_ids)
    v_full, u_full = gather_factors(both, v_bank.shape[0])
    proj_in = folder(activations, v_full)
    proj_out = folder(out_grads, u_full)
    scores = (proj_in * proj_out).reshape(tok_rows, queries, RANK).sum(axis=2)
    total = total_over(jnp.sum(scores * scores, axis=0), TOK, n)
    scale = jnp.sqrt(total / (tok_rows * n) + 1e-06)
    return scores * (1.0 / scale)[None, :]


def split_mesh(mesh):
    grp, tok = mesh.devices.shape
    assert tok % 8 == 0
    return Mesh(mesh.devices.reshape(grp, tok // 8, 4, 2), ("grp",) + TOK)


def solution(mesh):
    rows = P(TOK, None)
    return jax.shard_map(
        on_device,
        mesh=split_mesh(mesh),
        in_specs=(rows, rows, rows, rows, P("grp")),
        out_specs=P(TOK, "grp"),
        check_vma=False,
    )
```
